256 devices in a mesh: lon: 64 (over z, x, y_lo), lat: 4 (over y_hi, core).
Axes of the slice: x: 4, y: 4 (y_hi: 2, y_lo: 2; y = y_hi * 2 + y_lo), z: 8, core: 2. Of those that a mesh axis runs over, the one named last changes fastest.
Arguments:
- queries: bfloat16 [64, 1024, 512], P('lat', 'lon'), may hold values from -160 to 160
- keys: bfloat16 [64, 1024, 512], P('lat', 'lon'), may hold values from -4 to 4
- values: bfloat16 [64, 1024, 512], P('lat', 'lon'), may hold values from -6 to 6
- d_out: bfloat16 [64, 1024, 512], P('lat', 'lon'), may hold values from -6 to 6
Outputs:
- d_queries: bfloat16 [64, 1024, 512], P('lat', 'lon')
- d_keys: bfloat16 [64, 1024, 512], P('lat', 'lon')
- d_values: bfloat16 [64, 1024, 512], P('lat', 'lon')
The draws below stay inside these ranges and needn't reach their ends.
All inputs are finite; a program needn't handle non-finite values.
Results may differ from the reference program's by a relative error of at most 0.012.
Values may be sent and summed in bfloat16 or wider, within the bound.
No kernel may reach another device: no remote copies, remote signals or barrier semaphores. Data moves between devices by JAX's collectives and lax.ppermute only.
A program may use at most 256 MiB of HBM per device.

```python
import math
import jax
import jax.numpy as jnp
from jax import lax

D = 512
HEADS = 8
ROWS = 64
COLS = 1024


def joint_fields(key):
    base_keys = jnp.clip(jax.random.normal(jax.random.fold_in(key, 101), (ROWS, COLS, D), jnp.float32), -4.0, 4.0)
    base_queries = jnp.clip(jax.random.normal(jax.random.fold_in(key, 102), (ROWS, COLS, D), jnp.float32), -4.0, 4.0)
    keys_out = base_keys
    queries_out = base_queries
    return (queries_out, keys_out)


def draw_queries(key, part):
    return joint_fields(key)[0].astype(jnp.bfloat16)


def draw_keys(key, part):
    return joint_fields(key)[1].astype(jnp.bfloat16)


def steps_of(own_key, dims, cuts, smallest, top_value):
    loudness = 1.0
    for axis_at, parts in cuts:
        steps = jax.random.uniform(jax.random.fold_in(jax.random.fold_in(own_key, 6), axis_at), (parts,), jnp.float32, smallest / len(cuts), top_value / len(cuts))
        loudness = loudness * jnp.repeat(jnp.exp(steps), dims[axis_at] // parts).reshape((-1,) + (1,) * (len(dims) - 1 - axis_at))
    return loudness


def gaussian(own_key, dims, scale, most, cuts=(), kind=jnp.bfloat16):
    factor_of = steps_of(own_key, dims, cuts, -0.22, 0.18) if cuts else 1.0
    array = jax.random.normal(own_key, dims, jnp.float32) * scale * factor_of
    return jnp.minimum(jnp.maximum(array, -most), most).astype(kind)


def setup_inputs(seed: int = 0) -> dict:
    key_list = jax.random.split(jax.random.key(seed), 5)
    queries = draw_queries(jax.random.fold_in(key_list[4], 71), 0)
    keys = draw_keys(jax.random.fold_in(key_list[4], 71), 0)
    values = gaussian(key_list[2], (ROWS, COLS, D), 1.0, 6.0, ((0, 4), (1, 64)))
    d_out = gaussian(key_list[3], (ROWS, COLS, D), 1.0, 6.0, ((0, 4), (1, 64)))
    return dict(queries=queries, keys=keys, values=values, d_out=d_out)


neg_fill = -1e+30

def window_keep(first_row, total_rows):
    shape = (8, 8, 20, 20)
    query_row = lax.broadcasted_iota(jnp.int32, shape, 0)
    query_col = lax.broadcasted_iota(jnp.int32, shape, 1)
    key_row = lax.broadcasted_iota(jnp.int32, shape, 2)
    key_col = lax.broadcasted_iota(jnp.int32, shape, 3)
    region_top = jnp.clip(first_row - 6, 0, total_rows - 20).astype(jnp.int32)
    start = jnp.clip(first_row + query_row - 6, 0, total_rows - 13)
    global_key = region_top + key_row
    keep = (global_key >= start) & (global_key < start + 13) & (key_col >= query_col) & (key_col <= query_col + 12)
    return (keep.reshape(64, 400), region_top)

def to_regions(slab, tiles):
    width = slab.shape[-1]
    padded = jnp.pad(slab, ((0, 0), (0, 4), (0, 0)))
    blocks = padded.reshape(20, tiles + 2, 8, width)
    joined = jnp.concatenate([blocks[:, :tiles], blocks[:, 1:tiles + 1], blocks[:, 2:, :4]], axis=2)
    return joined.transpose(1, 0, 2, 3).reshape(tiles, 400, width)

def from_regions(grads, tiles):
    width = grads.shape[-1]
    split = grads.reshape(tiles, 20, 20, width).transpose(1, 0, 2, 3)
    first = jnp.pad(split[:, :, 0:8], ((0, 0), (0, 2), (0, 0), (0, 0)))
    second = jnp.pad(split[:, :, 8:16], ((0, 0), (1, 1), (0, 0), (0, 0)))
    third = jnp.pad(split[:, :, 16:20], ((0, 0), (2, 0), (0, 4), (0, 0)))
    total = (first + second + third).reshape(20, 8 * tiles + 16, width)
    return total[:, :8 * tiles + 12]

def row_grads(q_rows, do_rows, k_slab, v_slab, keep):
    width = q_rows.shape[-1]
    tiles = q_rows.shape[1] // 8
    head_dim = width // HEADS
    scale = 1.0 / math.sqrt(head_dim)

    def tiled(rows):
        return rows.reshape(8, tiles, 8, width).transpose(1, 0, 2, 3).reshape(tiles, 64, HEADS, head_dim)
    query_tiles = tiled(q_rows).astype(jnp.float32)
    grad_tiles = tiled(do_rows).astype(jnp.float32)
    key_tiles = to_regions(k_slab, tiles).reshape(tiles, 400, HEADS, head_dim).astype(jnp.float32)
    value_tiles = to_regions(v_slab, tiles).reshape(tiles, 400, HEADS, head_dim).astype(jnp.float32)
    scores = jnp.einsum('nqhd,nkhd->nhqk', query_tiles, key_tiles) * scale
    scores = jnp.where(keep, scores, neg_fill)
    probs = jnp.exp(scores - lax.optimization_barrier(jnp.max(scores, axis=-1, keepdims=True)))
    probs = probs / lax.optimization_barrier(jnp.sum(probs, axis=-1, keepdims=True))
    weights = lax.optimization_barrier(probs.astype(jnp.bfloat16)).astype(jnp.float32)
    attended = jnp.einsum('nhqk,nkhd->nqhd', weights, value_tiles)
    dprobs = jnp.einsum('nqhd,nkhd->nhqk', grad_tiles, value_tiles)
    delta = lax.optimization_barrier(jnp.sum(grad_tiles * attended, axis=-1)).transpose(0, 2, 1)
    dscores = probs * (dprobs - delta[..., None]) * scale
    dscores = lax.optimization_barrier(dscores.astype(jnp.bfloat16)).astype(jnp.float32)
    d_query = jnp.einsum('nhqk,nkhd->nqhd', dscores, key_tiles).reshape(tiles, 8, 8, width)
    d_query = d_query.transpose(1, 0, 2, 3).reshape(8, 8 * tiles, width)
    d_key = jnp.einsum('nhqk,nqhd->nkhd', dscores, query_tiles).reshape(tiles, 400, width)
    d_value = jnp.einsum('nhqk,nqhd->nkhd', weights, grad_tiles).reshape(tiles, 400, width)
    return (d_query, jnp.stack([from_regions(d_key, tiles), from_regions(d_value, tiles)]))

def reference(queries, keys, values, d_out):
    total_rows, total_cols, width = queries.shape
    pair = jnp.stack([keys, values])
    pair = jnp.concatenate([pair[:, :, total_cols - 6:], pair, pair[:, :, :6]], axis=2)

    def step(acc, index):
        first_row = (index * 8).astype(jnp.int32)
        keep, top = window_keep(first_row, total_rows)
        q_rows = lax.dynamic_slice_in_dim(queries, first_row, 8, 0)
        do_rows = lax.dynamic_slice_in_dim(d_out, first_row, 8, 0)
        slab = lax.dynamic_slice_in_dim(pair, top, 20, 1)
        d_query, grads = row_grads(q_rows, do_rows, slab[0], slab[1], keep)
        current = lax.dynamic_slice_in_dim(acc, top, 20, 1)
        acc = lax.dynamic_update_slice_in_dim(acc, current + grads, top, 1)
        return (acc, d_query)
    start_acc = jnp.zeros((2, total_rows, total_cols + 12, width), jnp.float32)
    acc, dq_rows = lax.scan(step, start_acc, jnp.arange(total_rows // 8, dtype=jnp.int32))
    folded = acc[:, :, 6:total_cols + 6]
    folded = folded.at[:, :, :6].add(acc[:, :, total_cols + 6:])
    folded = folded.at[:, :, total_cols - 6:].add(acc[:, :, :6])
    d_queries = dq_rows.reshape(total_rows, total_cols, width).astype(jnp.bfloat16)
    return (d_queries, folded[0].astype(jnp.bfloat16), folded[1].astype(jnp.bfloat16))
```

```python
import functools
import math

import jax
import jax.numpy as jnp
from jax import lax
from jax.experimental import pallas as pl
from jax.experimental.pallas import tpu as pltpu
from jax.sharding import PartitionSpec as P

HEADS = 8
HALF = 6
WIN = 2 * HALF + 1
PAD_COLS = 4
LANES = 128


DIRS = [(dr, dc) for dr in (-1, 0, 1) for dc in (-1, 0, 1) if (dr, dc) != (0, 0)]


def own_slice(d, n):
    return {-1: slice(n - HALF, n), 0: slice(0, n), 1: slice(0, HALF)}[d]


def halo_slice(d, n):
    return {-1: slice(0, HALF), 0: slice(HALF, HALF + n), 1: slice(HALF + n, 2 * HALF + n)}[d]


def shift(x, dr, dc):
    n_lat = lax.axis_size("lat")
    n_lon = lax.axis_size("lon")
    pairs = []
    for a in range(n_lat):
        if not 0 <= a + dr < n_lat:
            continue
        for b in range(n_lon):
            pairs.append((b * n_lat + a, ((b + dc) % n_lon) * n_lat + a + dr))
    return lax.ppermute(x, ("lon", "lat"), pairs)


def gather_halo(pair):
    _, rows, cols, _ = pair.shape
    got = {}
    for dr, dc in DIRS:
        piece = pair[:, own_slice(dr, rows), own_slice(dc, cols)]
        got[(dr, dc)] = shift(piece, -dr, -dc)
    got[(0, 0)] = pair
    bands = []
    for dr in (-1, 0, 1):
        band = jnp.concatenate([got[(dr, dc)] for dc in (-1, 0, 1)], axis=2)
        bands.append(band)
    ext = jnp.concatenate(bands, axis=1)
    return jnp.pad(ext, ((0, 0), (0, 0), (0, PAD_COLS), (0, 0)))


def return_halo(grads, rows, cols):
    owned = grads[:, HALF : HALF + rows, HALF : HALF + cols]
    for dr, dc in DIRS:
        piece = grads[:, halo_slice(dr, rows), halo_slice(dc, cols)].astype(jnp.bfloat16)
        got = shift(piece, dr, dc).astype(jnp.float32)
        rs, cs = own_slice(dr, rows), own_slice(dc, cols)
        widths = ((0, 0), (rs.start, rows - rs.stop), (cs.start, cols - cs.stop), (0, 0))
        owned = owned + jnp.pad(got, widths)
    return owned


def attention_kernel(first_ref, q_ref, do_ref, kv_ref, dq_ref, dkv_ref, bias_ref, *, cols, ext_cols, total_rows, head_dim):
    nq = q_ref.shape[0]
    nk = kv_ref.shape[1]
    scale = 1.0 / math.sqrt(head_dim)
    f32 = jnp.float32
    nt = (((1,), (1,)), ((), ()))

    @pl.when(pl.program_id(0) == 0)
    def _():
        first = first_ref[0]
        qi = lax.broadcasted_iota(jnp.int32, (nq, nk), 0)
        ki = lax.broadcasted_iota(jnp.int32, (nq, nk), 1)
        r = lax.shift_right_logical(qi, cols.bit_length() - 1)
        c = lax.bitwise_and(qi, cols - 1)
        i = lax.shift_right_logical(ki, ext_cols.bit_length() - 1)
        j = lax.bitwise_and(ki, ext_cols - 1)
        start = jnp.minimum(jnp.maximum(first + r - HALF, 0), total_rows - WIN) - first + HALF
        keep = (j >= c) & (j <= c + 2 * HALF) & (i >= start) & (i <= start + 2 * HALF)
        bias_ref[...] = jnp.where(keep, 0.0, -1e30).astype(f32)

    q2 = q_ref[...]
    do2 = do_ref[...]
    k2 = kv_ref[0]
    v2 = kv_ref[1]
    lane = lax.broadcasted_iota(jnp.int32, (1, LANES), 1)
    lo = lane < head_dim
    outs = []
    for sel in (lo, jnp.logical_not(lo)):
        qh = jnp.where(sel, q2, jnp.zeros_like(q2))
        doh = jnp.where(sel, do2, jnp.zeros_like(do2))
        s = lax.dot_general(qh, k2, nt, preferred_element_type=f32) * scale + bias_ref[...]
        m = jnp.max(s, axis=1, keepdims=True)
        p = jnp.exp(s - m)
        l = jnp.sum(p, axis=1, keepdims=True)
        probs = p * (1.0 / l)
        w = probs.astype(jnp.bfloat16)
        att = jnp.dot(w, v2, preferred_element_type=f32)
        dp = lax.dot_general(doh, v2, nt, preferred_element_type=f32)
        delta = jnp.sum(jnp.where(sel, do2.astype(f32) * att, 0.0), axis=1, keepdims=True)
        dsf = probs * (dp - delta) * scale
        ds = dsf.astype(jnp.bfloat16)
        dq = jnp.dot(ds, k2, preferred_element_type=f32)
        dk = jnp.dot(dsf.T.astype(jnp.bfloat16), q2, preferred_element_type=f32)
        dv = jnp.dot(probs.T.astype(jnp.bfloat16), do2, preferred_element_type=f32)
        outs.append((dq, dk, dv))
    (dq_a, dk_a, dv_a), (dq_b, dk_b, dv_b) = outs
    dq_ref[...] = jnp.where(lo, dq_a, dq_b).astype(dq_ref.dtype)
    dkv_ref[0] = jnp.where(lo, dk_a, dk_b)
    dkv_ref[1] = jnp.where(lo, dv_a, dv_b)


def local_grads(first_row, q, do, kv, cols, ext_cols, total_rows):
    nq, width = q.shape
    nk = kv.shape[1]
    head_dim = width // HEADS
    steps = width // LANES
    kern = functools.partial(
        attention_kernel, cols=cols, ext_cols=ext_cols, total_rows=total_rows, head_dim=head_dim
    )
    grid_spec = pltpu.PrefetchScalarGridSpec(
        num_scalar_prefetch=1,
        grid=(steps,),
        in_specs=[
            pl.BlockSpec((nq, LANES), lambda p, f: (0, p)),
            pl.BlockSpec((nq, LANES), lambda p, f: (0, p)),
            pl.BlockSpec((2, nk, LANES), lambda p, f: (0, 0, p)),
        ],
        out_specs=[
            pl.BlockSpec((nq, LANES), lambda p, f: (0, p)),
            pl.BlockSpec((2, nk, LANES), lambda p, f: (0, 0, p)),
        ],
        scratch_shapes=[pltpu.VMEM((nq, nk), jnp.float32)],
    )
    flops = 2 * nq * nk * LANES * 6 * HEADS
    cost = pl.CostEstimate(
        flops=flops,
        transcendentals=nq * nk * HEADS,
        bytes_accessed=2 * nq * width * 2 + 2 * nk * width * 2 + nq * width * 2 + 2 * nk * width * 4,
    )
    return pl.pallas_call(
        kern,
        grid_spec=grid_spec,
        out_shape=[
            jax.ShapeDtypeStruct((nq, width), jnp.bfloat16),
            jax.ShapeDtypeStruct((2, nk, width), jnp.float32),
        ],
        compiler_params=pltpu.CompilerParams(
            dimension_semantics=("arbitrary",), vmem_limit_bytes=48 * 1024 * 1024
        ),
        cost_estimate=cost,
    )(first_row, q, do, kv)


def per_device(queries, keys, values, d_out):
    rows, cols, width = queries.shape
    total_rows = rows * lax.axis_size("lat")
    first_row = (lax.axis_index("lat") * rows).astype(jnp.int32).reshape(1)
    pair = jnp.stack([keys, values])
    ext = gather_halo(pair)
    ext_rows, ext_cols = ext.shape[1], ext.shape[2]
    kv = ext.reshape(2, ext_rows * ext_cols, width)
    dq, dkv = local_grads(
        first_row,
        queries.reshape(rows * cols, width),
        d_out.reshape(rows * cols, width),
        kv,
        cols,
        ext_cols,
        total_rows,
    )
    grads = dkv.reshape(2, ext_rows, ext_cols, width)[:, :, : ext_cols - PAD_COLS]
    owned = return_halo(grads, rows, cols)
    return (
        dq.reshape(rows, cols, width),
        owned[0].astype(jnp.bfloat16),
        owned[1].astype(jnp.bfloat16),
    )


def solution(mesh):
    spec = P("lat", "lon", None)
    return jax.shard_map(
        per_device, mesh=mesh, in_specs=(spec,) * 4, out_specs=(spec,) * 3, check_vma=False
    )
```

```python
import functools
import math

import jax
import jax.numpy as jnp
from jax import lax
from jax.experimental import pallas as pl
from jax.experimental.pallas import tpu as pltpu
from jax.sharding import PartitionSpec as P

HEADS = 8
HALF = 6
WIN = 2 * HALF + 1
PAD_COLS = 4
LANES = 128


def own_slice(d, n):
    return {-1: slice(n - HALF, n), 0: slice(0, n), 1: slice(0, HALF)}[d]


def halo_slice(d, n):
    return {-1: slice(0, HALF), 0: slice(HALF, HALF + n), 1: slice(HALF + n, 2 * HALF + n)}[d]


def shift(x, dr, dc):
    n_lat = lax.axis_size("lat")
    n_lon = lax.axis_size("lon")
    pairs = []
    for a in range(n_lat):
        if not 0 <= a + dr < n_lat:
            continue
        for b in range(n_lon):
            pairs.append((b * n_lat + a, ((b + dc) % n_lon) * n_lat + a + dr))
    return lax.ppermute(x, ("lon", "lat"), pairs)


def gather_halo(pair):
    _, rows, cols, _ = pair.shape
    left = shift(pair[:, :, own_slice(-1, cols)], 0, 1)
    right = shift(pair[:, :, own_slice(1, cols)], 0, -1)
    wide = jnp.concatenate([left, pair, right], axis=2)
    top = shift(wide[:, own_slice(-1, rows)], 1, 0)
    bottom = shift(wide[:, own_slice(1, rows)], -1, 0)
    ext = jnp.concatenate([top, wide, bottom], axis=1)
    return jnp.pad(ext, ((0, 0), (0, 0), (0, PAD_COLS), (0, 0)))


def return_halo(grads, rows, cols):
    band = grads[:, HALF : HALF + rows]
    up = shift(grads[:, halo_slice(-1, rows)].astype(jnp.bfloat16), -1, 0).astype(jnp.float32)
    down = shift(grads[:, halo_slice(1, rows)].astype(jnp.bfloat16), 1, 0).astype(jnp.float32)
    band = band + jnp.pad(up, ((0, 0), (rows - HALF, 0), (0, 0), (0, 0)))
    band = band + jnp.pad(down, ((0, 0), (0, rows - HALF), (0, 0), (0, 0)))
    owned = band[:, :, HALF : HALF + cols]
    west = shift(band[:, :, halo_slice(-1, cols)].astype(jnp.bfloat16), 0, -1).astype(jnp.float32)
    east = shift(band[:, :, halo_slice(1, cols)].astype(jnp.bfloat16), 0, 1).astype(jnp.float32)
    owned = owned + jnp.pad(west, ((0, 0), (0, 0), (cols - HALF, 0), (0, 0)))
    owned = owned + jnp.pad(east, ((0, 0), (0, 0), (0, cols - HALF), (0, 0)))
    return owned


def attention_kernel(first_ref, q_ref, do_ref, kv_ref, dq_ref, dkv_ref, bias_ref, *, cols, ext_cols, total_rows, head_dim):
    nq = q_ref.shape[0]
    nk = kv_ref.shape[1]
    scale = 1.0 / math.sqrt(head_dim)
    f32 = jnp.float32
    nt = (((1,), (1,)), ((), ()))

    @pl.when(pl.program_id(0) == 0)
    def _():
        first = first_ref[0]
        qi = lax.broadcasted_iota(jnp.int32, (nq, nk), 0)
        ki = lax.broadcasted_iota(jnp.int32, (nq, nk), 1)
        r = lax.shift_right_logical(qi, cols.bit_length() - 1)
        c = lax.bitwise_and(qi, cols - 1)
        i = lax.shift_right_logical(ki, ext_cols.bit_length() - 1)
        j = lax.bitwise_and(ki, ext_cols - 1)
        start = jnp.minimum(jnp.maximum(first + r - HALF, 0), total_rows - WIN) - first + HALF
        keep = (j >= c) & (j <= c + 2 * HALF) & (i >= start) & (i <= start + 2 * HALF)
        bias_ref[...] = jnp.where(keep, 0.0, -1e30).astype(f32)

    q2 = q_ref[...]
    do2 = do_ref[...]
    k2 = kv_ref[0]
    v2 = kv_ref[1]
    lane = lax.broadcasted_iota(jnp.int32, (1, LANES), 1)
    lo = lane < head_dim
    outs = []
    for sel in (lo, jnp.logical_not(lo)):
        qh = jnp.where(sel, q2, jnp.zeros_like(q2))
        doh = jnp.where(sel, do2, jnp.zeros_like(do2))
        s = lax.dot_general(qh, k2, nt, preferred_element_type=f32) * scale + bias_ref[...]
        m = jnp.max(s, axis=1, keepdims=True)
        p = jnp.exp(s - m)
        l = jnp.sum(p, axis=1, keepdims=True)
        probs = p * (1.0 / l)
        w = probs.astype(jnp.bfloat16)
        att = jnp.dot(w, v2, preferred_element_type=f32)
        dp = lax.dot_general(doh, v2, nt, preferred_element_type=f32)
        delta = jnp.sum(jnp.where(sel, do2.astype(f32) * att, 0.0), axis=1, keepdims=True)
        dsf = probs * (dp - delta) * scale
        ds = dsf.astype(jnp.bfloat16)
        dq = jnp.dot(ds, k2, preferred_element_type=f32)
        dk = jnp.dot(dsf.T.astype(jnp.bfloat16), q2, preferred_element_type=f32)
        dv = jnp.dot(probs.T.astype(jnp.bfloat16), do2, preferred_element_type=f32)
        outs.append((dq, dk, dv))
    (dq_a, dk_a, dv_a), (dq_b, dk_b, dv_b) = outs
    dq_ref[...] = jnp.where(lo, dq_a, dq_b).astype(dq_ref.dtype)
    dkv_ref[0] = jnp.where(lo, dk_a, dk_b)
    dkv_ref[1] = jnp.where(lo, dv_a, dv_b)


def local_grads(first_row, q, do, kv, cols, ext_cols, total_rows):
    nq, width = q.shape
    nk = kv.shape[1]
    head_dim = width // HEADS
    steps = width // LANES
    kern = functools.partial(
        attention_kernel, cols=cols, ext_cols=ext_cols, total_rows=total_rows, head_dim=head_dim
    )
    grid_spec = pltpu.PrefetchScalarGridSpec(
        num_scalar_prefetch=1,
        grid=(steps,),
        in_specs=[
            pl.BlockSpec((nq, LANES), lambda p, f: (0, p)),
            pl.BlockSpec((nq, LANES), lambda p, f: (0, p)),
            pl.BlockSpec((2, nk, LANES), lambda p, f: (0, 0, p)),
        ],
        out_specs=[
            pl.BlockSpec((nq, LANES), lambda p, f: (0, p)),
            pl.BlockSpec((2, nk, LANES), lambda p, f: (0, 0, p)),
        ],
        scratch_shapes=[pltpu.VMEM((nq, nk), jnp.float32)],
    )
    flops = 2 * nq * nk * LANES * 6 * HEADS
    cost = pl.CostEstimate(
        flops=flops,
        transcendentals=nq * nk * HEADS,
        bytes_accessed=2 * nq * width * 2 + 2 * nk * width * 2 + nq * width * 2 + 2 * nk * width * 4,
    )
    return pl.pallas_call(
        kern,
        grid_spec=grid_spec,
        out_shape=[
            jax.ShapeDtypeStruct((nq, width), jnp.bfloat16),
            jax.ShapeDtypeStruct((2, nk, width), jnp.float32),
        ],
        compiler_params=pltpu.CompilerParams(
            dimension_semantics=("arbitrary",), vmem_limit_bytes=48 * 1024 * 1024
        ),
        cost_estimate=cost,
    )(first_row, q, do, kv)


def per_device(queries, keys, values, d_out):
    rows, cols, width = queries.shape
    total_rows = rows * lax.axis_size("lat")
    first_row = (lax.axis_index("lat") * rows).astype(jnp.int32).reshape(1)
    pair = jnp.stack([keys, values])
    ext = gather_halo(pair)
    ext_rows, ext_cols = ext.shape[1], ext.shape[2]
    kv = ext.reshape(2, ext_rows * ext_cols, width)
    dq, dkv = local_grads(
        first_row,
        queries.reshape(rows * cols, width),
        d_out.reshape(rows * cols, width),
        kv,
        cols,
        ext_cols,
        total_rows,
    )
    grads = dkv.reshape(2, ext_rows, ext_cols, width)[:, :, : ext_cols - PAD_COLS]
    owned = return_halo(grads, rows, cols)
    return (
        dq.reshape(rows, cols, width),
        owned[0].astype(jnp.bfloat16),
        owned[1].astype(jnp.bfloat16),
    )


def solution(mesh):
    spec = P("lat", "lon", None)
    return jax.shard_map(
        per_device, mesh=mesh, in_specs=(spec,) * 4, out_specs=(spec,) * 3, check_vma=False
    )
```

```python
import functools
import math

import jax
import jax.numpy as jnp
from jax import lax
from jax.experimental import pallas as pl
from jax.experimental.pallas import tpu as pltpu
from jax.sharding import PartitionSpec as P

HEADS = 8
HALF = 6
WIN = 2 * HALF + 1
PAD_COLS = 4
LANES = 128


def own_slice(d, n):
    return {-1: slice(n - HALF, n), 0: slice(0, n), 1: slice(0, HALF)}[d]


def halo_slice(d, n):
    return {-1: slice(0, HALF), 0: slice(HALF, HALF + n), 1: slice(HALF + n, 2 * HALF + n)}[d]


def shift(x, dr, dc):
    n_lat = lax.axis_size("lat")
    n_lon = lax.axis_size("lon")
    pairs = []
    for a in range(n_lat):
        if not 0 <= a + dr < n_lat:
            continue
        for b in range(n_lon):
            pairs.append((b * n_lat + a, ((b + dc) % n_lon) * n_lat + a + dr))
    return lax.ppermute(x, ("lon", "lat"), pairs)


def gather_halo(pair):
    _, rows, cols, _ = pair.shape
    left = shift(pair[:, :, own_slice(-1, cols)], 0, 1)
    right = shift(pair[:, :, own_slice(1, cols)], 0, -1)
    wide = jnp.concatenate([left, pair, right], axis=2)
    top = shift(wide[:, own_slice(-1, rows)], 1, 0)
    bottom = shift(wide[:, own_slice(1, rows)], -1, 0)
    ext = jnp.concatenate([top, wide, bottom], axis=1)
    return jnp.pad(ext, ((0, 0), (0, 0), (0, PAD_COLS), (0, 0)))


def return_halo(grads, rows, cols):
    band = grads[:, HALF : HALF + rows]
    up = shift(grads[:, halo_slice(-1, rows)].astype(jnp.bfloat16), -1, 0).astype(jnp.float32)
    down = shift(grads[:, halo_slice(1, rows)].astype(jnp.bfloat16), 1, 0).astype(jnp.float32)
    band = band + jnp.pad(up, ((0, 0), (rows - HALF, 0), (0, 0), (0, 0)))
    band = band + jnp.pad(down, ((0, 0), (0, rows - HALF), (0, 0), (0, 0)))
    owned = band[:, :, HALF : HALF + cols]
    west = shift(band[:, :, halo_slice(-1, cols)].astype(jnp.bfloat16), 0, -1).astype(jnp.float32)
    east = shift(band[:, :, halo_slice(1, cols)].astype(jnp.bfloat16), 0, 1).astype(jnp.float32)
    owned = owned + jnp.pad(west, ((0, 0), (0, 0), (cols - HALF, 0), (0, 0)))
    owned = owned + jnp.pad(east, ((0, 0), (0, 0), (0, cols - HALF), (0, 0)))
    return owned


def attention_kernel(first_ref, q_ref, do_ref, kv_ref, dq_ref, dkv_ref, bias_ref, *, cols, ext_cols, total_rows, head_dim):
    nq = q_ref.shape[0]
    nk = kv_ref.shape[1]
    scale = 1.0 / math.sqrt(head_dim)
    f32 = jnp.float32
    nt = (((1,), (1,)), ((), ()))

    @pl.when(pl.program_id(0) == 0)
    def _():
        first = first_ref[0]
        qi = lax.broadcasted_iota(jnp.int32, (nq, nk), 0)
        ki = lax.broadcasted_iota(jnp.int32, (nq, nk), 1)
        r = lax.shift_right_logical(qi, cols.bit_length() - 1)
        c = lax.bitwise_and(qi, cols - 1)
        i = lax.shift_right_logical(ki, ext_cols.bit_length() - 1)
        j = lax.bitwise_and(ki, ext_cols - 1)
        start = jnp.minimum(jnp.maximum(first + r - HALF, 0), total_rows - WIN) - first + HALF
        keep = (j >= c) & (j <= c + 2 * HALF) & (i >= start) & (i <= start + 2 * HALF)
        bias_ref[...] = jnp.where(keep, 0.0, -1e30).astype(f32)

    q2 = q_ref[...]
    do2 = do_ref[...]
    k2 = kv_ref[0]
    v2 = kv_ref[1]
    qt = q2.astype(f32).T.astype(jnp.bfloat16)
    dot_t = do2.astype(f32).T.astype(jnp.bfloat16)
    lane = lax.broadcasted_iota(jnp.int32, (1, LANES), 1)
    lo = lane < head_dim
    outs = []
    for h, sel in enumerate((lo, jnp.logical_not(lo))):
        qh = jnp.where(sel, q2, jnp.zeros_like(q2))
        doh = jnp.where(sel, do2, jnp.zeros_like(do2))
        s = lax.dot_general(qh, k2, nt, preferred_element_type=f32) * scale + bias_ref[...]
        m = jnp.max(s, axis=1, keepdims=True)
        p = jnp.exp(s - m)
        l = jnp.sum(p, axis=1, keepdims=True)
        probs = p * (1.0 / l)
        w = probs.astype(jnp.bfloat16)
        att = jnp.dot(w, v2, preferred_element_type=f32)
        dp = lax.dot_general(doh, v2, nt, preferred_element_type=f32)
        delta = jnp.sum(jnp.where(sel, do2.astype(f32) * att, 0.0), axis=1, keepdims=True)
        ds = (probs * (dp - delta) * scale).astype(jnp.bfloat16)
        dq = jnp.dot(ds, k2, preferred_element_type=f32)
        dims = slice(h * head_dim, (h + 1) * head_dim)
        dkt = jnp.dot(qt[dims], ds, preferred_element_type=f32)
        dvt = jnp.dot(dot_t[dims], w, preferred_element_type=f32)
        outs.append((dq, dkt, dvt))
    (dq_a, dk_a, dv_a), (dq_b, dk_b, dv_b) = outs
    dq_ref[...] = jnp.where(lo, dq_a, dq_b).astype(dq_ref.dtype)
    dkv_ref[0] = jnp.concatenate([dk_a, dk_b], axis=0).T
    dkv_ref[1] = jnp.concatenate([dv_a, dv_b], axis=0).T


def local_grads(first_row, q, do, kv, cols, ext_cols, total_rows):
    nq, width = q.shape
    nk = kv.shape[1]
    head_dim = width // HEADS
    steps = width // LANES
    kern = functools.partial(
        attention_kernel, cols=cols, ext_cols=ext_cols, total_rows=total_rows, head_dim=head_dim
    )
    grid_spec = pltpu.PrefetchScalarGridSpec(
        num_scalar_prefetch=1,
        grid=(steps,),
        in_specs=[
            pl.BlockSpec((nq, LANES), lambda p, f: (0, p)),
            pl.BlockSpec((nq, LANES), lambda p, f: (0, p)),
            pl.BlockSpec((2, nk, LANES), lambda p, f: (0, 0, p)),
        ],
        out_specs=[
            pl.BlockSpec((nq, LANES), lambda p, f: (0, p)),
            pl.BlockSpec((2, nk, LANES), lambda p, f: (0, 0, p)),
        ],
        scratch_shapes=[pltpu.VMEM((nq, nk), jnp.float32)],
    )
    flops = 2 * nq * nk * LANES * 6 * HEADS
    cost = pl.CostEstimate(
        flops=flops,
        transcendentals=nq * nk * HEADS,
        bytes_accessed=2 * nq * width * 2 + 2 * nk * width * 2 + nq * width * 2 + 2 * nk * width * 4,
    )
    return pl.pallas_call(
        kern,
        grid_spec=grid_spec,
        out_shape=[
            jax.ShapeDtypeStruct((nq, width), jnp.bfloat16),
            jax.ShapeDtypeStruct((2, nk, width), jnp.float32),
        ],
        compiler_params=pltpu.CompilerParams(
            dimension_semantics=("arbitrary",), vmem_limit_bytes=48 * 1024 * 1024
        ),
        cost_estimate=cost,
    )(first_row, q, do, kv)


def per_device(queries, keys, values, d_out):
    rows, cols, width = queries.shape
    total_rows = rows * lax.axis_size("lat")
    first_row = (lax.axis_index("lat") * rows).astype(jnp.int32).reshape(1)
    pair = jnp.stack([keys, values])
    ext = gather_halo(pair)
    ext_rows, ext_cols = ext.shape[1], ext.shape[2]
    kv = ext.reshape(2, ext_rows * ext_cols, width)
    dq, dkv = local_grads(
        first_row,
        queries.reshape(rows * cols, width),
        d_out.reshape(rows * cols, width),
        kv,
        cols,
        ext_cols,
        total_rows,
    )
    grads = dkv.reshape(2, ext_rows, ext_cols, width)[:, :, : ext_cols - PAD_COLS]
    owned = return_halo(grads, rows, cols)
    return (
        dq.reshape(rows, cols, width),
        owned[0].astype(jnp.bfloat16),
        owned[1].astype(jnp.bfloat16),
    )


def solution(mesh):
    spec = P("lat", "lon", None)
    return jax.shard_map(
        per_device, mesh=mesh, in_specs=(spec,) * 4, out_specs=(spec,) * 3, check_vma=False
    )
```

```python
import functools
import math

import jax
import jax.numpy as jnp
from jax import lax
from jax.experimental import pallas as pl
from jax.experimental.pallas import tpu as pltpu
from jax.sharding import PartitionSpec as P

HEADS = 8
HALF = 6
WIN = 2 * HALF + 1
PAD_COLS = 4
LANES = 128


def own_slice(d, n):
    return {-1: slice(n - HALF, n), 0: slice(0, n), 1: slice(0, HALF)}[d]


def halo_slice(d, n):
    return {-1: slice(0, HALF), 0: slice(HALF, HALF + n), 1: slice(HALF + n, 2 * HALF + n)}[d]


def shift(x, dr, dc):
    n_lat = lax.axis_size("lat")
    n_lon = lax.axis_size("lon")
    pairs = []
    for a in range(n_lat):
        if not 0 <= a + dr < n_lat:
            continue
        for b in range(n_lon):
            pairs.append((b * n_lat + a, ((b + dc) % n_lon) * n_lat + a + dr))
    flat = x.reshape(-1, x.shape[-1])
    return lax.ppermute(flat, ("lon", "lat"), pairs).reshape(x.shape)


def gather_halo(pair):
    _, rows, cols, _ = pair.shape
    left = shift(pair[:, :, own_slice(-1, cols)], 0, 1)
    right = shift(pair[:, :, own_slice(1, cols)], 0, -1)
    wide = jnp.concatenate([left, pair, right], axis=2)
    top = shift(wide[:, own_slice(-1, rows)], 1, 0)
    bottom = shift(wide[:, own_slice(1, rows)], -1, 0)
    ext = jnp.concatenate([top, wide, bottom], axis=1)
    return jnp.pad(ext, ((0, 0), (0, 0), (0, PAD_COLS), (0, 0)))


def return_halo(grads, rows, cols):
    band = grads[:, HALF : HALF + rows]
    up = shift(grads[:, halo_slice(-1, rows)].astype(jnp.bfloat16), -1, 0).astype(jnp.float32)
    down = shift(grads[:, halo_slice(1, rows)].astype(jnp.bfloat16), 1, 0).astype(jnp.float32)
    band = band + jnp.pad(up, ((0, 0), (rows - HALF, 0), (0, 0), (0, 0)))
    band = band + jnp.pad(down, ((0, 0), (0, rows - HALF), (0, 0), (0, 0)))
    owned = band[:, :, HALF : HALF + cols]
    west = shift(band[:, :, halo_slice(-1, cols)].astype(jnp.bfloat16), 0, -1).astype(jnp.float32)
    east = shift(band[:, :, halo_slice(1, cols)].astype(jnp.bfloat16), 0, 1).astype(jnp.float32)
    owned = owned + jnp.pad(west, ((0, 0), (0, 0), (cols - HALF, 0), (0, 0)))
    owned = owned + jnp.pad(east, ((0, 0), (0, 0), (0, cols - HALF), (0, 0)))
    return owned


def attention_kernel(first_ref, q_ref, do_ref, kv_ref, dq_ref, dkv_ref, bias_ref, *, cols, ext_cols, total_rows, head_dim):
    nq = q_ref.shape[0]
    nk = kv_ref.shape[1]
    scale = 1.0 / math.sqrt(head_dim)
    f32 = jnp.float32
    nt = (((1,), (1,)), ((), ()))

    @pl.when(pl.program_id(0) == 0)
    def _():
        first = first_ref[0]
        qi = lax.broadcasted_iota(jnp.int32, (nq, nk), 0)
        ki = lax.broadcasted_iota(jnp.int32, (nq, nk), 1)
        r = lax.shift_right_logical(qi, cols.bit_length() - 1)
        c = lax.bitwise_and(qi, cols - 1)
        i = lax.shift_right_logical(ki, ext_cols.bit_length() - 1)
        j = lax.bitwise_and(ki, ext_cols - 1)
        start = jnp.minimum(jnp.maximum(first + r - HALF, 0), total_rows - WIN) - first + HALF
        keep = (j >= c) & (j <= c + 2 * HALF) & (i >= start) & (i <= start + 2 * HALF)
        bias_ref[...] = jnp.where(keep, 0.0, -1e30).astype(f32)

    q2 = q_ref[...]
    do2 = do_ref[...]
    k2 = kv_ref[0]
    v2 = kv_ref[1]
    qt = q2.astype(f32).T.astype(jnp.bfloat16)
    dot_t = do2.astype(f32).T.astype(jnp.bfloat16)
    lane = lax.broadcasted_iota(jnp.int32, (1, LANES), 1)
    lo = lane < head_dim
    outs = []
    for h, sel in enumerate((lo, jnp.logical_not(lo))):
        qh = jnp.where(sel, q2, jnp.zeros_like(q2))
        doh = jnp.where(sel, do2, jnp.zeros_like(do2))
        s = lax.dot_general(qh, k2, nt, preferred_element_type=f32) * scale + bias_ref[...]
        m = jnp.max(s, axis=1, keepdims=True)
        p = jnp.exp(s - m)
        l = jnp.sum(p, axis=1, keepdims=True)
        probs = p * (1.0 / l)
        w = probs.astype(jnp.bfloat16)
        att = jnp.dot(w, v2, preferred_element_type=f32)
        dp = lax.dot_general(doh, v2, nt, preferred_element_type=f32)
        delta = jnp.sum(jnp.where(sel, do2.astype(f32) * att, 0.0), axis=1, keepdims=True)
        ds = (probs * (dp - delta) * scale).astype(jnp.bfloat16)
        dq = jnp.dot(ds, k2, preferred_element_type=f32)
        dims = slice(h * head_dim, (h + 1) * head_dim)
        dkt = jnp.dot(qt[dims], ds, preferred_element_type=f32)
        dvt = jnp.dot(dot_t[dims], w, preferred_element_type=f32)
        outs.append((dq, dkt, dvt))
    (dq_a, dk_a, dv_a), (dq_b, dk_b, dv_b) = outs
    dq_ref[...] = jnp.where(lo, dq_a, dq_b).astype(dq_ref.dtype)
    dkv_ref[0] = jnp.concatenate([dk_a, dk_b], axis=0).T
    dkv_ref[1] = jnp.concatenate([dv_a, dv_b], axis=0).T


def local_grads(first_row, q, do, kv, cols, ext_cols, total_rows):
    nq, width = q.shape
    nk = kv.shape[1]
    head_dim = width // HEADS
    steps = width // LANES
    kern = functools.partial(
        attention_kernel, cols=cols, ext_cols=ext_cols, total_rows=total_rows, head_dim=head_dim
    )
    grid_spec = pltpu.PrefetchScalarGridSpec(
        num_scalar_prefetch=1,
        grid=(steps,),
        in_specs=[
            pl.BlockSpec((nq, LANES), lambda p, f: (0, p)),
            pl.BlockSpec((nq, LANES), lambda p, f: (0, p)),
            pl.BlockSpec((2, nk, LANES), lambda p, f: (0, 0, p)),
        ],
        out_specs=[
            pl.BlockSpec((nq, LANES), lambda p, f: (0, p)),
            pl.BlockSpec((2, nk, LANES), lambda p, f: (0, 0, p)),
        ],
        scratch_shapes=[pltpu.VMEM((nq, nk), jnp.float32)],
    )
    flops = 2 * nq * nk * LANES * 6 * HEADS
    cost = pl.CostEstimate(
        flops=flops,
        transcendentals=nq * nk * HEADS,
        bytes_accessed=2 * nq * width * 2 + 2 * nk * width * 2 + nq * width * 2 + 2 * nk * width * 4,
    )
    return pl.pallas_call(
        kern,
        grid_spec=grid_spec,
        out_shape=[
            jax.ShapeDtypeStruct((nq, width), jnp.bfloat16),
            jax.ShapeDtypeStruct((2, nk, width), jnp.float32),
        ],
        compiler_params=pltpu.CompilerParams(
            dimension_semantics=("arbitrary",), vmem_limit_bytes=48 * 1024 * 1024
        ),
        cost_estimate=cost,
    )(first_row, q, do, kv)


def per_device(queries, keys, values, d_out):
    rows, cols, width = queries.shape
    total_rows = rows * lax.axis_size("lat")
    first_row = (lax.axis_index("lat") * rows).astype(jnp.int32).reshape(1)
    pair = jnp.stack([keys, values])
    ext = gather_halo(pair)
    ext_rows, ext_cols = ext.shape[1], ext.shape[2]
    kv = ext.reshape(2, ext_rows * ext_cols, width)
    dq, dkv = local_grads(
        first_row,
        queries.reshape(rows * cols, width),
        d_out.reshape(rows * cols, width),
        kv,
        cols,
        ext_cols,
        total_rows,
    )
    grads = dkv.reshape(2, ext_rows, ext_cols, width)[:, :, : ext_cols - PAD_COLS]
    owned = return_halo(grads, rows, cols)
    return (
        dq.reshape(rows, cols, width),
        owned[0].astype(jnp.bfloat16),
        owned[1].astype(jnp.bfloat16),
    )


def solution(mesh):
    spec = P("lat", "lon", None)
    return jax.shard_map(
        per_device, mesh=mesh, in_specs=(spec,) * 4, out_specs=(spec,) * 3, check_vma=False
    )
```

```python
import functools
import math

import jax
import jax.numpy as jnp
from jax import lax
from jax.experimental import pallas as pl
from jax.experimental.pallas import tpu as pltpu
from jax.sharding import PartitionSpec as P

HEADS = 8
HALF = 6
WIN = 2 * HALF + 1
PAD_COLS = 4
LANES = 128


def own_slice(d, n):
    return {-1: slice(n - HALF, n), 0: slice(0, n), 1: slice(0, HALF)}[d]


def halo_slice(d, n):
    return {-1: slice(0, HALF), 0: slice(HALF, HALF + n), 1: slice(HALF + n, 2 * HALF + n)}[d]


def shift(x, dr, dc):
    n_lat = lax.axis_size("lat")
    n_lon = lax.axis_size("lon")
    pairs = []
    for a in range(n_lat):
        if not 0 <= a + dr < n_lat:
            continue
        for b in range(n_lon):
            pairs.append((b * n_lat + a, ((b + dc) % n_lon) * n_lat + a + dr))
    flat = x.reshape(-1, x.shape[-1])
    return lax.ppermute(flat, ("lon", "lat"), pairs).reshape(x.shape)


def gather_halo(pair, after=None):
    _, rows, cols, _ = pair.shape
    left = shift(pair[:, :, own_slice(-1, cols)], 0, 1)
    right = shift(pair[:, :, own_slice(1, cols)], 0, -1)
    wide = jnp.concatenate([left, pair, right], axis=2)
    top = shift(wide[:, own_slice(-1, rows)], 1, 0)
    bottom = shift(wide[:, own_slice(1, rows)], -1, 0)
    if after is not None:
        top, wide, bottom, _ = lax.optimization_barrier((top, wide, bottom, after))
    ext = jnp.concatenate([top, wide, bottom], axis=1)
    return jnp.pad(ext, ((0, 0), (0, 0), (0, PAD_COLS), (0, 0)))


def return_halo(grads, rows, cols):
    band = grads[:, HALF : HALF + rows]
    up = shift(grads[:, halo_slice(-1, rows)].astype(jnp.bfloat16), -1, 0).astype(jnp.float32)
    down = shift(grads[:, halo_slice(1, rows)].astype(jnp.bfloat16), 1, 0).astype(jnp.float32)
    band = band + jnp.pad(up, ((0, 0), (rows - HALF, 0), (0, 0), (0, 0)))
    band = band + jnp.pad(down, ((0, 0), (0, rows - HALF), (0, 0), (0, 0)))
    owned = band[:, :, HALF : HALF + cols]
    west = shift(band[:, :, halo_slice(-1, cols)].astype(jnp.bfloat16), 0, -1).astype(jnp.float32)
    east = shift(band[:, :, halo_slice(1, cols)].astype(jnp.bfloat16), 0, 1).astype(jnp.float32)
    owned = owned + jnp.pad(west, ((0, 0), (0, 0), (cols - HALF, 0), (0, 0)))
    owned = owned + jnp.pad(east, ((0, 0), (0, 0), (0, cols - HALF), (0, 0)))
    return owned


def attention_kernel(first_ref, q_ref, do_ref, kv_ref, dq_ref, dkv_ref, bias_ref, *, cols, ext_cols, total_rows, head_dim):
    nq = q_ref.shape[0]
    nk = kv_ref.shape[1]
    scale = 1.0 / math.sqrt(head_dim)
    f32 = jnp.float32
    nt = (((1,), (1,)), ((), ()))

    @pl.when(pl.program_id(0) == 0)
    def _():
        first = first_ref[0]
        qi = lax.broadcasted_iota(jnp.int32, (nq, nk), 0)
        ki = lax.broadcasted_iota(jnp.int32, (nq, nk), 1)
        r = lax.shift_right_logical(qi, cols.bit_length() - 1)
        c = lax.bitwise_and(qi, cols - 1)
        i = lax.shift_right_logical(ki, ext_cols.bit_length() - 1)
        j = lax.bitwise_and(ki, ext_cols - 1)
        start = jnp.minimum(jnp.maximum(first + r - HALF, 0), total_rows - WIN) - first + HALF
        keep = (j >= c) & (j <= c + 2 * HALF) & (i >= start) & (i <= start + 2 * HALF)
        bias_ref[...] = jnp.where(keep, 0.0, -1e30).astype(f32)

    q2 = q_ref[...]
    do2 = do_ref[...]
    k2 = kv_ref[0]
    v2 = kv_ref[1]
    qt = q2.astype(f32).T.astype(jnp.bfloat16)
    dot_t = do2.astype(f32).T.astype(jnp.bfloat16)
    lane = lax.broadcasted_iota(jnp.int32, (1, LANES), 1)
    lo = lane < head_dim
    outs = []
    for h, sel in enumerate((lo, jnp.logical_not(lo))):
        qh = jnp.where(sel, q2, jnp.zeros_like(q2))
        doh = jnp.where(sel, do2, jnp.zeros_like(do2))
        s = lax.dot_general(qh, k2, nt, preferred_element_type=f32) * scale + bias_ref[...]
        m = jnp.max(s, axis=1, keepdims=True)
        p = jnp.exp(s - m)
        l = jnp.sum(p, axis=1, keepdims=True)
        probs = p * (1.0 / l)
        w = probs.astype(jnp.bfloat16)
        att = jnp.dot(w, v2, preferred_element_type=f32)
        dp = lax.dot_general(doh, v2, nt, preferred_element_type=f32)
        delta = jnp.sum(jnp.where(sel, do2.astype(f32) * att, 0.0), axis=1, keepdims=True)
        ds = (probs * (dp - delta) * scale).astype(jnp.bfloat16)
        dq = jnp.dot(ds, k2, preferred_element_type=f32)
        dims = slice(h * head_dim, (h + 1) * head_dim)
        dkt = jnp.dot(qt[dims], ds, preferred_element_type=f32)
        dvt = jnp.dot(dot_t[dims], w, preferred_element_type=f32)
        outs.append((dq, dkt, dvt))
    (dq_a, dk_a, dv_a), (dq_b, dk_b, dv_b) = outs
    dq_ref[...] = jnp.where(lo, dq_a, dq_b).astype(dq_ref.dtype)
    dkv_ref[0] = jnp.concatenate([dk_a, dk_b], axis=0).T
    dkv_ref[1] = jnp.concatenate([dv_a, dv_b], axis=0).T


def local_grads(first_row, q, do, kv, cols, ext_cols, total_rows, heads):
    nq, width = q.shape
    nk = kv.shape[1]
    head_dim = width // heads
    steps = width // LANES
    kern = functools.partial(
        attention_kernel, cols=cols, ext_cols=ext_cols, total_rows=total_rows, head_dim=head_dim
    )
    grid_spec = pltpu.PrefetchScalarGridSpec(
        num_scalar_prefetch=1,
        grid=(steps,),
        in_specs=[
            pl.BlockSpec((nq, LANES), lambda p, f: (0, p)),
            pl.BlockSpec((nq, LANES), lambda p, f: (0, p)),
            pl.BlockSpec((2, nk, LANES), lambda p, f: (0, 0, p)),
        ],
        out_specs=[
            pl.BlockSpec((nq, LANES), lambda p, f: (0, p)),
            pl.BlockSpec((2, nk, LANES), lambda p, f: (0, 0, p)),
        ],
        scratch_shapes=[pltpu.VMEM((nq, nk), jnp.float32)],
    )
    flops = 2 * nq * nk * LANES * 6 * heads
    cost = pl.CostEstimate(
        flops=flops,
        transcendentals=nq * nk * heads,
        bytes_accessed=2 * nq * width * 2 + 2 * nk * width * 2 + nq * width * 2 + 2 * nk * width * 4,
    )
    return pl.pallas_call(
        kern,
        grid_spec=grid_spec,
        out_shape=[
            jax.ShapeDtypeStruct((nq, width), jnp.bfloat16),
            jax.ShapeDtypeStruct((2, nk, width), jnp.float32),
        ],
        compiler_params=pltpu.CompilerParams(
            dimension_semantics=("arbitrary",), vmem_limit_bytes=48 * 1024 * 1024
        ),
        cost_estimate=cost,
    )(first_row, q, do, kv)


CHUNKS = 2


def per_device(queries, keys, values, d_out):
    rows, cols, width = queries.shape
    total_rows = rows * lax.axis_size("lat")
    first_row = (lax.axis_index("lat") * rows).astype(jnp.int32).reshape(1)
    part = width // CHUNKS
    dqs, dks, dvs = [], [], []
    after = None
    for chunk in range(CHUNKS):
        lanes = slice(chunk * part, (chunk + 1) * part)
        pair = jnp.stack([keys[:, :, lanes], values[:, :, lanes]])
        ext = gather_halo(pair, after)
        ext_rows, ext_cols = ext.shape[1], ext.shape[2]
        kv = ext.reshape(2, ext_rows * ext_cols, part)
        dq, dkv = local_grads(
            first_row,
            queries[:, :, lanes].reshape(rows * cols, part),
            d_out[:, :, lanes].reshape(rows * cols, part),
            kv,
            cols,
            ext_cols,
            total_rows,
            HEADS // CHUNKS,
        )
        after = dq
        grads = dkv.reshape(2, ext_rows, ext_cols, part)[:, :, : ext_cols - PAD_COLS]
        owned = return_halo(grads, rows, cols)
        dqs.append(dq.reshape(rows, cols, part))
        dks.append(owned[0])
        dvs.append(owned[1])
    return (
        jnp.concatenate(dqs, axis=-1),
        jnp.concatenate(dks, axis=-1).astype(jnp.bfloat16),
        jnp.concatenate(dvs, axis=-1).astype(jnp.bfloat16),
    )


def solution(mesh):
    spec = P("lat", "lon", None)
    return jax.shard_map(
        per_device, mesh=mesh, in_specs=(spec,) * 4, out_specs=(spec,) * 3, check_vma=False
    )
```

```python
import functools
import math

import jax
import jax.numpy as jnp
from jax import lax
from jax.experimental import pallas as pl
from jax.experimental.pallas import tpu as pltpu
from jax.sharding import PartitionSpec as P

HEADS = 8
HALF = 6
WIN = 2 * HALF + 1
PAD_COLS = 4
LANES = 128


def own_slice(d, n):
    return {-1: slice(n - HALF, n), 0: slice(0, n), 1: slice(0, HALF)}[d]


def halo_slice(d, n):
    return {-1: slice(0, HALF), 0: slice(HALF, HALF + n), 1: slice(HALF + n, 2 * HALF + n)}[d]


def shift(x, dr, dc):
    n_lat = lax.axis_size("lat")
    n_lon = lax.axis_size("lon")
    pairs = []
    for a in range(n_lat):
        if not 0 <= a + dr < n_lat:
            continue
        for b in range(n_lon):
            pairs.append((b * n_lat + a, ((b + dc) % n_lon) * n_lat + a + dr))
    flat = x.reshape(-1, x.shape[-1])
    return lax.ppermute(flat, ("lon", "lat"), pairs).reshape(x.shape)


def gather_halo(pair):
    _, rows, cols, _ = pair.shape
    top = shift(pair[:, own_slice(-1, rows)], 1, 0)
    bottom = shift(pair[:, own_slice(1, rows)], -1, 0)
    tall = jnp.concatenate([top, pair, bottom], axis=1)
    left = shift(tall[:, :, own_slice(-1, cols)], 0, 1)
    right = shift(tall[:, :, own_slice(1, cols)], 0, -1)
    ext = jnp.concatenate([left, tall, right], axis=2)
    return jnp.pad(ext, ((0, 0), (0, 0), (0, PAD_COLS), (0, 0)))


def return_halo(grads, rows, cols):
    band = grads[:, :, HALF : HALF + cols]
    west = shift(grads[:, :, halo_slice(-1, cols)].astype(jnp.bfloat16), 0, -1).astype(jnp.float32)
    east = shift(grads[:, :, halo_slice(1, cols)].astype(jnp.bfloat16), 0, 1).astype(jnp.float32)
    band = band + jnp.pad(west, ((0, 0), (0, 0), (cols - HALF, 0), (0, 0)))
    band = band + jnp.pad(east, ((0, 0), (0, 0), (0, cols - HALF), (0, 0)))
    owned = band[:, HALF : HALF + rows]
    up = shift(band[:, halo_slice(-1, rows)].astype(jnp.bfloat16), -1, 0).astype(jnp.float32)
    down = shift(band[:, halo_slice(1, rows)].astype(jnp.bfloat16), 1, 0).astype(jnp.float32)
    owned = owned + jnp.pad(up, ((0, 0), (rows - HALF, 0), (0, 0), (0, 0)))
    owned = owned + jnp.pad(down, ((0, 0), (0, rows - HALF), (0, 0), (0, 0)))
    return owned


def attention_kernel(first_ref, q_ref, do_ref, kv_ref, dq_ref, dkv_ref, bias_ref, *, cols, ext_cols, total_rows, head_dim):
    nq = q_ref.shape[0]
    nk = kv_ref.shape[1]
    scale = 1.0 / math.sqrt(head_dim)
    f32 = jnp.float32
    nt = (((1,), (1,)), ((), ()))

    @pl.when(pl.program_id(0) == 0)
    def _():
        first = first_ref[0]
        qi = lax.broadcasted_iota(jnp.int32, (nq, nk), 0)
        ki = lax.broadcasted_iota(jnp.int32, (nq, nk), 1)
        r = lax.shift_right_logical(qi, cols.bit_length() - 1)
        c = lax.bitwise_and(qi, cols - 1)
        i = lax.shift_right_logical(ki, ext_cols.bit_length() - 1)
        j = lax.bitwise_and(ki, ext_cols - 1)
        start = jnp.minimum(jnp.maximum(first + r - HALF, 0), total_rows - WIN) - first + HALF
        keep = (j >= c) & (j <= c + 2 * HALF) & (i >= start) & (i <= start + 2 * HALF)
        bias_ref[...] = jnp.where(keep, 0.0, -1e30).astype(f32)

    q2 = q_ref[...]
    do2 = do_ref[...]
    k2 = kv_ref[0]
    v2 = kv_ref[1]
    qt = q2.astype(f32).T.astype(jnp.bfloat16)
    dot_t = do2.astype(f32).T.astype(jnp.bfloat16)
    lane = lax.broadcasted_iota(jnp.int32, (1, LANES), 1)
    lo = lane < head_dim
    outs = []
    for h, sel in enumerate((lo, jnp.logical_not(lo))):
        qh = jnp.where(sel, q2, jnp.zeros_like(q2))
        doh = jnp.where(sel, do2, jnp.zeros_like(do2))
        s = lax.dot_general(qh, k2, nt, preferred_element_type=f32) * scale + bias_ref[...]
        m = jnp.max(s, axis=1, keepdims=True)
        p = jnp.exp(s - m)
        l = jnp.sum(p, axis=1, keepdims=True)
        probs = p * (1.0 / l)
        w = probs.astype(jnp.bfloat16)
        att = jnp.dot(w, v2, preferred_element_type=f32)
        dp = lax.dot_general(doh, v2, nt, preferred_element_type=f32)
        delta = jnp.sum(jnp.where(sel, do2.astype(f32) * att, 0.0), axis=1, keepdims=True)
        ds = (probs * (dp - delta) * scale).astype(jnp.bfloat16)
        dq = jnp.dot(ds, k2, preferred_element_type=f32)
        dims = slice(h * head_dim, (h + 1) * head_dim)
        dkt = jnp.dot(qt[dims], ds, preferred_element_type=f32)
        dvt = jnp.dot(dot_t[dims], w, preferred_element_type=f32)
        outs.append((dq, dkt, dvt))
    (dq_a, dk_a, dv_a), (dq_b, dk_b, dv_b) = outs
    dq_ref[...] = jnp.where(lo, dq_a, dq_b).astype(dq_ref.dtype)
    dkv_ref[0] = jnp.concatenate([dk_a, dk_b], axis=0).T
    dkv_ref[1] = jnp.concatenate([dv_a, dv_b], axis=0).T


def local_grads(first_row, q, do, kv, cols, ext_cols, total_rows):
    nq, width = q.shape
    nk = kv.shape[1]
    head_dim = width // HEADS
    steps = width // LANES
    kern = functools.partial(
        attention_kernel, cols=cols, ext_cols=ext_cols, total_rows=total_rows, head_dim=head_dim
    )
    grid_spec = pltpu.PrefetchScalarGridSpec(
        num_scalar_prefetch=1,
        grid=(steps,),
        in_specs=[
            pl.BlockSpec((nq, LANES), lambda p, f: (0, p)),
            pl.BlockSpec((nq, LANES), lambda p, f: (0, p)),
            pl.BlockSpec((2, nk, LANES), lambda p, f: (0, 0, p)),
        ],
        out_specs=[
            pl.BlockSpec((nq, LANES), lambda p, f: (0, p)),
            pl.BlockSpec((2, nk, LANES), lambda p, f: (0, 0, p)),
        ],
        scratch_shapes=[pltpu.VMEM((nq, nk), jnp.float32)],
    )
    flops = 2 * nq * nk * LANES * 6 * HEADS
    cost = pl.CostEstimate(
        flops=flops,
        transcendentals=nq * nk * HEADS,
        bytes_accessed=2 * nq * width * 2 + 2 * nk * width * 2 + nq * width * 2 + 2 * nk * width * 4,
    )
    return pl.pallas_call(
        kern,
        grid_spec=grid_spec,
        out_shape=[
            jax.ShapeDtypeStruct((nq, width), jnp.bfloat16),
            jax.ShapeDtypeStruct((2, nk, width), jnp.float32),
        ],
        compiler_params=pltpu.CompilerParams(
            dimension_semantics=("arbitrary",), vmem_limit_bytes=48 * 1024 * 1024
        ),
        cost_estimate=cost,
    )(first_row, q, do, kv)


def per_device(queries, keys, values, d_out):
    rows, cols, width = queries.shape
    total_rows = rows * lax.axis_size("lat")
    first_row = (lax.axis_index("lat") * rows).astype(jnp.int32).reshape(1)
    pair = jnp.stack([keys, values])
    ext = gather_halo(pair)
    ext_rows, ext_cols = ext.shape[1], ext.shape[2]
    kv = ext.reshape(2, ext_rows * ext_cols, width)
    dq, dkv = local_grads(
        first_row,
        queries.reshape(rows * cols, width),
        d_out.reshape(rows * cols, width),
        kv,
        cols,
        ext_cols,
        total_rows,
    )
    grads = dkv.reshape(2, ext_rows, ext_cols, width)[:, :, : ext_cols - PAD_COLS]
    owned = return_halo(grads, rows, cols)
    return (
        dq.reshape(rows, cols, width),
        owned[0].astype(jnp.bfloat16),
        owned[1].astype(jnp.bfloat16),
    )


def solution(mesh):
    spec = P("lat", "lon", None)
    return jax.shard_map(
        per_device, mesh=mesh, in_specs=(spec,) * 4, out_specs=(spec,) * 3, check_vma=False
    )
```

```python
import functools
import math

import jax
import jax.numpy as jnp
from jax import lax
from jax.experimental import pallas as pl
from jax.experimental.pallas import tpu as pltpu
from jax.sharding import PartitionSpec as P

HEADS = 8
HALF = 6
WIN = 2 * HALF + 1
PAD_COLS = 4
LANES = 128


def own_slice(d, n):
    return {-1: slice(n - HALF, n), 0: slice(0, n), 1: slice(0, HALF)}[d]


def halo_slice(d, n):
    return {-1: slice(0, HALF), 0: slice(HALF, HALF + n), 1: slice(HALF + n, 2 * HALF + n)}[d]


def shift(x, dr, dc):
    n_lat = lax.axis_size("lat")
    n_lon = lax.axis_size("lon")
    pairs = []
    for a in range(n_lat):
        if not 0 <= a + dr < n_lat:
            continue
        for b in range(n_lon):
            pairs.append((b * n_lat + a, ((b + dc) % n_lon) * n_lat + a + dr))
    flat = x.reshape(-1, x.shape[-1])
    return lax.ppermute(flat, ("lon", "lat"), pairs).reshape(x.shape)


def gather_halo(pair):
    _, rows, cols, _ = pair.shape
    left = shift(pair[:, :, own_slice(-1, cols)], 0, 1)
    right = shift(pair[:, :, own_slice(1, cols)], 0, -1)
    wide = jnp.concatenate([left, pair, right], axis=2)
    top = shift(wide[:, own_slice(-1, rows)], 1, 0)
    bottom = shift(wide[:, own_slice(1, rows)], -1, 0)
    ext = jnp.concatenate([top, wide, bottom], axis=1)
    return jnp.pad(ext, ((0, 0), (0, 0), (0, PAD_COLS), (0, 0)))


def return_halo(grads, rows, cols):
    band = grads[:, HALF : HALF + rows]
    up = shift(grads[:, halo_slice(-1, rows)].astype(jnp.bfloat16), -1, 0).astype(jnp.float32)
    down = shift(grads[:, halo_slice(1, rows)].astype(jnp.bfloat16), 1, 0).astype(jnp.float32)
    band = band + jnp.pad(up, ((0, 0), (rows - HALF, 0), (0, 0), (0, 0)))
    band = band + jnp.pad(down, ((0, 0), (0, rows - HALF), (0, 0), (0, 0)))
    owned = band[:, :, HALF : HALF + cols]
    west = shift(band[:, :, halo_slice(-1, cols)].astype(jnp.bfloat16), 0, -1).astype(jnp.float32)
    east = shift(band[:, :, halo_slice(1, cols)].astype(jnp.bfloat16), 0, 1).astype(jnp.float32)
    owned = owned + jnp.pad(west, ((0, 0), (0, 0), (cols - HALF, 0), (0, 0)))
    owned = owned + jnp.pad(east, ((0, 0), (0, 0), (0, cols - HALF), (0, 0)))
    return owned


def window_start(first, row, total_rows):
    return jnp.minimum(jnp.maximum(first + row - HALF, 0), total_rows - WIN) - first + HALF


def attention_kernel(first_ref, q_ref, do_ref, kv_ref, dq_ref, dkv_ref, bias_ref, *, cols, ext_cols, total_rows, head_dim):
    nq = q_ref.shape[0]
    nk = kv_ref.shape[1]
    rows = nq // cols
    half = rows // 2
    bq = half * cols
    bk = (half + 2 * HALF) * ext_cols
    shift_k = half * ext_cols
    scale = 1.0 / math.sqrt(head_dim)
    f32 = jnp.float32
    nt = (((1,), (1,)), ((), ()))
    first = first_ref[0]

    @pl.when(pl.program_id(0) == 0)
    def _():
        qi = lax.broadcasted_iota(jnp.int32, (bq, bk), 0)
        ki = lax.broadcasted_iota(jnp.int32, (bq, bk), 1)
        rr = lax.shift_right_logical(qi, cols.bit_length() - 1)
        c = lax.bitwise_and(qi, cols - 1)
        i = lax.shift_right_logical(ki, ext_cols.bit_length() - 1)
        j = lax.bitwise_and(ki, ext_cols - 1)
        for blk in range(2):
            start = window_start(first, blk * half + rr, total_rows) - blk * half
            keep = (j >= c) & (j <= c + 2 * HALF) & (i >= start) & (i <= start + 2 * HALF)
            bias_ref[blk] = jnp.where(keep, 0.0, -1e30).astype(f32)

    q2 = q_ref[...]
    do2 = do_ref[...]
    qt = q2.astype(f32).T.astype(jnp.bfloat16)
    dot_t = do2.astype(f32).T.astype(jnp.bfloat16)
    lane = lax.broadcasted_iota(jnp.int32, (1, LANES), 1)
    lo = lane < head_dim
    sels = (lo, jnp.logical_not(lo))
    chains = [(blk, h) for blk in range(2) for h in range(2)]
    qs = [slice(blk * bq, (blk + 1) * bq) for blk in range(2)]
    ks = [slice(blk * shift_k, blk * shift_k + bk) for blk in range(2)]
    k2 = [kv_ref[0, ks[blk], :] for blk in range(2)]
    v2 = [kv_ref[1, ks[blk], :] for blk in range(2)]
    qb = [q2[qs[blk]] for blk in range(2)]
    dob = [do2[qs[blk]] for blk in range(2)]
    sc = {}
    for blk, h in chains:
        qh = jnp.where(sels[h], qb[blk], jnp.zeros_like(qb[blk]))
        sc[blk, h] = lax.dot_general(qh, k2[blk], nt, preferred_element_type=f32)
    dps = {}
    for blk, h in chains:
        doh = jnp.where(sels[h], dob[blk], jnp.zeros_like(dob[blk]))
        dps[blk, h] = lax.dot_general(doh, v2[blk], nt, preferred_element_type=f32)
    probs, ws = {}, {}
    for blk, h in chains:
        s = sc[blk, h] * scale + bias_ref[blk]
        m = jnp.max(s, axis=1, keepdims=True)
        p = jnp.exp(s - m)
        l = jnp.sum(p, axis=1, keepdims=True)
        probs[blk, h] = p * (1.0 / l)
        ws[blk, h] = probs[blk, h].astype(jnp.bfloat16)
    atts = {}
    for blk, h in chains:
        atts[blk, h] = jnp.dot(ws[blk, h], v2[blk], preferred_element_type=f32)
    dss = {}
    for blk, h in chains:
        delta = jnp.sum(jnp.where(sels[h], dob[blk].astype(f32) * atts[blk, h], 0.0), axis=1, keepdims=True)
        dss[blk, h] = (probs[blk, h] * (dps[blk, h] - delta) * scale).astype(jnp.bfloat16)
    dqs = {}
    dkt = [[None, None], [None, None]]
    dvt = [[None, None], [None, None]]
    for blk, h in chains:
        dims = slice(h * head_dim, (h + 1) * head_dim)
        dqs[blk, h] = jnp.dot(dss[blk, h], k2[blk], preferred_element_type=f32)
        dkt[blk][h] = jnp.dot(qt[dims, qs[blk]], dss[blk, h], preferred_element_type=f32)
        dvt[blk][h] = jnp.dot(dot_t[dims, qs[blk]], ws[blk, h], preferred_element_type=f32)
    for blk in range(2):
        dq_ref[qs[blk], :] = jnp.where(lo, dqs[blk, 0], dqs[blk, 1]).astype(dq_ref.dtype)

    def joined(parts):
        heads = []
        for h in range(2):
            a, b = parts[0][h], parts[1][h]
            heads.append(
                jnp.concatenate(
                    [a[:, :shift_k], a[:, shift_k:] + b[:, : bk - shift_k], b[:, bk - shift_k :]], axis=1
                )
            )
        return jnp.concatenate(heads, axis=0).T

    dkv_ref[0] = joined(dkt)
    dkv_ref[1] = joined(dvt)


def local_grads(first_row, q, do, kv, cols, ext_cols, total_rows):
    nq, width = q.shape
    nk = kv.shape[1]
    head_dim = width // HEADS
    steps = width // LANES
    kern = functools.partial(
        attention_kernel, cols=cols, ext_cols=ext_cols, total_rows=total_rows, head_dim=head_dim
    )
    grid_spec = pltpu.PrefetchScalarGridSpec(
        num_scalar_prefetch=1,
        grid=(steps,),
        in_specs=[
            pl.BlockSpec((nq, LANES), lambda p, f: (0, p)),
            pl.BlockSpec((nq, LANES), lambda p, f: (0, p)),
            pl.BlockSpec((2, nk, LANES), lambda p, f: (0, 0, p)),
        ],
        out_specs=[
            pl.BlockSpec((nq, LANES), lambda p, f: (0, p)),
            pl.BlockSpec((2, nk, LANES), lambda p, f: (0, 0, p)),
        ],
        scratch_shapes=[pltpu.VMEM((2, nq // 2, nk - (nq // cols // 2) * ext_cols), jnp.float32)],
    )
    flops = 2 * nq * nk * LANES * 6 * HEADS
    cost = pl.CostEstimate(
        flops=flops,
        transcendentals=nq * nk * HEADS,
        bytes_accessed=2 * nq * width * 2 + 2 * nk * width * 2 + nq * width * 2 + 2 * nk * width * 4,
    )
    return pl.pallas_call(
        kern,
        grid_spec=grid_spec,
        out_shape=[
            jax.ShapeDtypeStruct((nq, width), jnp.bfloat16),
            jax.ShapeDtypeStruct((2, nk, width), jnp.float32),
        ],
        compiler_params=pltpu.CompilerParams(
            dimension_semantics=("arbitrary",), vmem_limit_bytes=48 * 1024 * 1024
        ),
        cost_estimate=cost,
    )(first_row, q, do, kv)


def per_device(queries, keys, values, d_out):
    rows, cols, width = queries.shape
    total_rows = rows * lax.axis_size("lat")
    first_row = (lax.axis_index("lat") * rows).astype(jnp.int32).reshape(1)
    pair = jnp.stack([keys, values])
    ext = gather_halo(pair)
    ext_rows, ext_cols = ext.shape[1], ext.shape[2]
    kv = ext.reshape(2, ext_rows * ext_cols, width)
    dq, dkv = local_grads(
        first_row,
        queries.reshape(rows * cols, width),
        d_out.reshape(rows * cols, width),
        kv,
        cols,
        ext_cols,
        total_rows,
    )
    grads = dkv.reshape(2, ext_rows, ext_cols, width)[:, :, : ext_cols - PAD_COLS]
    owned = return_halo(grads, rows, cols)
    return (
        dq.reshape(rows, cols, width),
        owned[0].astype(jnp.bfloat16),
        owned[1].astype(jnp.bfloat16),
    )


def solution(mesh):
    spec = P("lat", "lon", None)
    return jax.shard_map(
        per_device, mesh=mesh, in_specs=(spec,) * 4, out_specs=(spec,) * 3, check_vma=False
    )
```

```python
import functools
import math

import jax
import jax.numpy as jnp
from jax import lax
from jax.experimental import pallas as pl
from jax.experimental.pallas import tpu as pltpu
from jax.sharding import PartitionSpec as P

HEADS = 8
HALF = 6
WIN = 2 * HALF + 1
PAD_COLS = 4
LANES = 128
STEP_PAIRS = 2


def own_slice(d, n):
    return {-1: slice(n - HALF, n), 0: slice(0, n), 1: slice(0, HALF)}[d]


def halo_slice(d, n):
    return {-1: slice(0, HALF), 0: slice(HALF, HALF + n), 1: slice(HALF + n, 2 * HALF + n)}[d]


def shift(x, dr, dc):
    n_lat = lax.axis_size("lat")
    n_lon = lax.axis_size("lon")
    pairs = []
    for a in range(n_lat):
        if not 0 <= a + dr < n_lat:
            continue
        for b in range(n_lon):
            pairs.append((b * n_lat + a, ((b + dc) % n_lon) * n_lat + a + dr))
    flat = x.reshape(-1, x.shape[-1])
    return lax.ppermute(flat, ("lon", "lat"), pairs).reshape(x.shape)


def gather_halo(pair):
    _, rows, cols, _ = pair.shape
    left = shift(pair[:, :, own_slice(-1, cols)], 0, 1)
    right = shift(pair[:, :, own_slice(1, cols)], 0, -1)
    wide = jnp.concatenate([left, pair, right], axis=2)
    top = shift(wide[:, own_slice(-1, rows)], 1, 0)
    bottom = shift(wide[:, own_slice(1, rows)], -1, 0)
    ext = jnp.concatenate([top, wide, bottom], axis=1)
    return jnp.pad(ext, ((0, 0), (0, 0), (0, PAD_COLS), (0, 0)))


def return_halo(grads, rows, cols):
    band = grads[:, HALF : HALF + rows]
    up = shift(grads[:, halo_slice(-1, rows)].astype(jnp.bfloat16), -1, 0).astype(jnp.float32)
    down = shift(grads[:, halo_slice(1, rows)].astype(jnp.bfloat16), 1, 0).astype(jnp.float32)
    band = band + jnp.pad(up, ((0, 0), (rows - HALF, 0), (0, 0), (0, 0)))
    band = band + jnp.pad(down, ((0, 0), (0, rows - HALF), (0, 0), (0, 0)))
    owned = band[:, :, HALF : HALF + cols]
    west = shift(band[:, :, halo_slice(-1, cols)].astype(jnp.bfloat16), 0, -1).astype(jnp.float32)
    east = shift(band[:, :, halo_slice(1, cols)].astype(jnp.bfloat16), 0, 1).astype(jnp.float32)
    owned = owned + jnp.pad(west, ((0, 0), (0, 0), (cols - HALF, 0), (0, 0)))
    owned = owned + jnp.pad(east, ((0, 0), (0, 0), (0, cols - HALF), (0, 0)))
    return owned


def window_start(first, row, total_rows):
    return jnp.minimum(jnp.maximum(first + row - HALF, 0), total_rows - WIN) - first + HALF


def attention_kernel(first_ref, q_ref, do_ref, kv_ref, dq_ref, dkv_ref, bias_ref, *, cols, ext_cols, total_rows, head_dim):
    nq = q_ref.shape[0]
    nk = kv_ref.shape[1]
    rows = nq // cols
    half = rows // 2
    bq = half * cols
    bk = (half + 2 * HALF) * ext_cols
    shift_k = half * ext_cols
    scale = 1.0 / math.sqrt(head_dim)
    f32 = jnp.float32
    nt = (((1,), (1,)), ((), ()))
    first = first_ref[0]

    @pl.when(pl.program_id(0) == 0)
    def _():
        qi = lax.broadcasted_iota(jnp.int32, (bq, bk), 0)
        ki = lax.broadcasted_iota(jnp.int32, (bq, bk), 1)
        rr = lax.shift_right_logical(qi, cols.bit_length() - 1)
        c = lax.bitwise_and(qi, cols - 1)
        i = lax.shift_right_logical(ki, ext_cols.bit_length() - 1)
        j = lax.bitwise_and(ki, ext_cols - 1)
        for blk in range(2):
            start = window_start(first, blk * half + rr, total_rows) - blk * half
            keep = (j >= c) & (j <= c + 2 * HALF) & (i >= start) & (i <= start + 2 * HALF)
            bias_ref[blk] = jnp.where(keep, 0.0, -1e30).astype(f32)

    pairs = q_ref.shape[1] // LANES
    lane = lax.broadcasted_iota(jnp.int32, (1, LANES), 1)
    lo = lane < head_dim
    sels = (lo, jnp.logical_not(lo))
    chains = [(blk, g, h) for blk in range(2) for g in range(pairs) for h in range(2)]
    qs = [slice(blk * bq, (blk + 1) * bq) for blk in range(2)]
    ks = [slice(blk * shift_k, blk * shift_k + bk) for blk in range(2)]
    gl = [slice(g * LANES, (g + 1) * LANES) for g in range(pairs)]
    q2 = [q_ref[:, gl[g]] for g in range(pairs)]
    do2 = [do_ref[:, gl[g]] for g in range(pairs)]
    qt = [q2[g].astype(f32).T.astype(jnp.bfloat16) for g in range(pairs)]
    dot_t = [do2[g].astype(f32).T.astype(jnp.bfloat16) for g in range(pairs)]
    k2 = {(blk, g): kv_ref[0, ks[blk], gl[g]] for blk in range(2) for g in range(pairs)}
    v2 = {(blk, g): kv_ref[1, ks[blk], gl[g]] for blk in range(2) for g in range(pairs)}
    qb = {(blk, g): q2[g][qs[blk]] for blk in range(2) for g in range(pairs)}
    dob = {(blk, g): do2[g][qs[blk]] for blk in range(2) for g in range(pairs)}
    sc = {}
    for blk, g, h in chains:
        qh = jnp.where(sels[h], qb[blk, g], jnp.zeros_like(qb[blk, g]))
        sc[blk, g, h] = lax.dot_general(qh, k2[blk, g], nt, preferred_element_type=f32)
    dps = {}
    for blk, g, h in chains:
        doh = jnp.where(sels[h], dob[blk, g], jnp.zeros_like(dob[blk, g]))
        dps[blk, g, h] = lax.dot_general(doh, v2[blk, g], nt, preferred_element_type=f32)
    probs, ws = {}, {}
    for c in chains:
        s = sc[c] * scale + bias_ref[c[0]]
        m = jnp.max(s, axis=1, keepdims=True)
        p = jnp.exp(s - m)
        l = jnp.sum(p, axis=1, keepdims=True)
        probs[c] = p * (1.0 / l)
        ws[c] = probs[c].astype(jnp.bfloat16)
    atts = {}
    for blk, g, h in chains:
        atts[blk, g, h] = jnp.dot(ws[blk, g, h], v2[blk, g], preferred_element_type=f32)
    dss = {}
    for blk, g, h in chains:
        c = (blk, g, h)
        delta = jnp.sum(jnp.where(sels[h], dob[blk, g].astype(f32) * atts[c], 0.0), axis=1, keepdims=True)
        dss[c] = (probs[c] * (dps[c] - delta) * scale).astype(jnp.bfloat16)
    dqs, dkt, dvt = {}, {}, {}
    for blk, g, h in chains:
        c = (blk, g, h)
        dims = slice(h * head_dim, (h + 1) * head_dim)
        dqs[c] = jnp.dot(dss[c], k2[blk, g], preferred_element_type=f32)
        dkt[c] = jnp.dot(qt[g][dims, qs[blk]], dss[c], preferred_element_type=f32)
        dvt[c] = jnp.dot(dot_t[g][dims, qs[blk]], ws[c], preferred_element_type=f32)
    for blk in range(2):
        for g in range(pairs):
            dq_ref[qs[blk], gl[g]] = jnp.where(lo, dqs[blk, g, 0], dqs[blk, g, 1]).astype(dq_ref.dtype)

    def joined(parts, g):
        heads = []
        for h in range(2):
            a, b = parts[0, g, h], parts[1, g, h]
            heads.append(
                jnp.concatenate(
                    [a[:, :shift_k], a[:, shift_k:] + b[:, : bk - shift_k], b[:, bk - shift_k :]], axis=1
                )
            )
        return jnp.concatenate(heads, axis=0).T

    for g in range(pairs):
        dkv_ref[0, :, gl[g]] = joined(dkt, g)
        dkv_ref[1, :, gl[g]] = joined(dvt, g)


def local_grads(first_row, q, do, kv, cols, ext_cols, total_rows):
    nq, width = q.shape
    nk = kv.shape[1]
    head_dim = width // HEADS
    step_lanes = LANES * STEP_PAIRS
    steps = width // step_lanes
    kern = functools.partial(
        attention_kernel, cols=cols, ext_cols=ext_cols, total_rows=total_rows, head_dim=head_dim
    )
    grid_spec = pltpu.PrefetchScalarGridSpec(
        num_scalar_prefetch=1,
        grid=(steps,),
        in_specs=[
            pl.BlockSpec((nq, step_lanes), lambda p, f: (0, p)),
            pl.BlockSpec((nq, step_lanes), lambda p, f: (0, p)),
            pl.BlockSpec((2, nk, step_lanes), lambda p, f: (0, 0, p)),
        ],
        out_specs=[
            pl.BlockSpec((nq, step_lanes), lambda p, f: (0, p)),
            pl.BlockSpec((2, nk, step_lanes), lambda p, f: (0, 0, p)),
        ],
        scratch_shapes=[pltpu.VMEM((2, nq // 2, nk - (nq // cols // 2) * ext_cols), jnp.float32)],
    )
    flops = 2 * nq * nk * LANES * 6 * HEADS
    cost = pl.CostEstimate(
        flops=flops,
        transcendentals=nq * nk * HEADS,
        bytes_accessed=2 * nq * width * 2 + 2 * nk * width * 2 + nq * width * 2 + 2 * nk * width * 4,
    )
    return pl.pallas_call(
        kern,
        grid_spec=grid_spec,
        out_shape=[
            jax.ShapeDtypeStruct((nq, width), jnp.bfloat16),
            jax.ShapeDtypeStruct((2, nk, width), jnp.float32),
        ],
        compiler_params=pltpu.CompilerParams(
            dimension_semantics=("arbitrary",), vmem_limit_bytes=48 * 1024 * 1024
        ),
        cost_estimate=cost,
    )(first_row, q, do, kv)


def per_device(queries, keys, values, d_out):
    rows, cols, width = queries.shape
    total_rows = rows * lax.axis_size("lat")
    first_row = (lax.axis_index("lat") * rows).astype(jnp.int32).reshape(1)
    pair = jnp.stack([keys, values])
    ext = gather_halo(pair)
    ext_rows, ext_cols = ext.shape[1], ext.shape[2]
    kv = ext.reshape(2, ext_rows * ext_cols, width)
    dq, dkv = local_grads(
        first_row,
        queries.reshape(rows * cols, width),
        d_out.reshape(rows * cols, width),
        kv,
        cols,
        ext_cols,
        total_rows,
    )
    grads = dkv.reshape(2, ext_rows, ext_cols, width)[:, :, : ext_cols - PAD_COLS]
    owned = return_halo(grads, rows, cols)
    return (
        dq.reshape(rows, cols, width),
        owned[0].astype(jnp.bfloat16),
        owned[1].astype(jnp.bfloat16),
    )


def solution(mesh):
    spec = P("lat", "lon", None)
    return jax.shard_map(
        per_device, mesh=mesh, in_specs=(spec,) * 4, out_specs=(spec,) * 3, check_vma=False
    )
```

```python
import functools
import math

import jax
import jax.numpy as jnp
from jax import lax
from jax.experimental import pallas as pl
from jax.experimental.pallas import tpu as pltpu
from jax.sharding import PartitionSpec as P

HEADS = 8
HALF = 6
WIN = 2 * HALF + 1
PAD_COLS = 4
LANES = 128
STEP_PAIRS = 2


def own_slice(d, n):
    return {-1: slice(n - HALF, n), 0: slice(0, n), 1: slice(0, HALF)}[d]


def halo_slice(d, n):
    return {-1: slice(0, HALF), 0: slice(HALF, HALF + n), 1: slice(HALF + n, 2 * HALF + n)}[d]


def shift(x, dr, dc):
    n_lat = lax.axis_size("lat")
    n_lon = lax.axis_size("lon")
    pairs = []
    for a in range(n_lat):
        if not 0 <= a + dr < n_lat:
            continue
        for b in range(n_lon):
            pairs.append((b * n_lat + a, ((b + dc) % n_lon) * n_lat + a + dr))
    flat = x.reshape(-1, x.shape[-1])
    return lax.ppermute(flat, ("lon", "lat"), pairs).reshape(x.shape)


def gather_halo(pair):
    _, rows, cols, _ = pair.shape
    left = shift(pair[:, :, own_slice(-1, cols)], 0, 1)
    right = shift(pair[:, :, own_slice(1, cols)], 0, -1)
    wide = jnp.concatenate([left, pair, right], axis=2)
    top = shift(wide[:, own_slice(-1, rows)], 1, 0)
    bottom = shift(wide[:, own_slice(1, rows)], -1, 0)
    ext = jnp.concatenate([top, wide, bottom], axis=1)
    return jnp.pad(ext, ((0, 0), (0, 0), (0, PAD_COLS), (0, 0)))


def return_halo(grads, rows, cols):
    f32, bf16 = jnp.float32, jnp.bfloat16
    ec = slice(0, cols + 2 * HALF)
    up = shift(grads[:, halo_slice(-1, rows), ec].astype(bf16), -1, 0)
    down = shift(grads[:, halo_slice(1, rows), ec].astype(bf16), 1, 0)

    def band(g, u, d, cs):
        b = g[:, HALF : HALF + rows, cs]
        b = b + jnp.pad(u[:, :, cs].astype(f32), ((0, 0), (rows - HALF, 0), (0, 0), (0, 0)))
        return b + jnp.pad(d[:, :, cs].astype(f32), ((0, 0), (0, rows - HALF), (0, 0), (0, 0)))

    west_piece = band(grads, up, down, halo_slice(-1, cols)).astype(bf16)
    east_piece = band(grads, up, down, halo_slice(1, cols)).astype(bf16)
    west_piece, east_piece, grads, up, down = lax.optimization_barrier((west_piece, east_piece, grads, up, down))
    west = shift(west_piece, 0, -1)
    east = shift(east_piece, 0, 1)
    centre = band(grads, up, down, halo_slice(0, cols))
    outs = []
    for i in range(2):
        o = centre[i] + jnp.pad(west[i].astype(f32), ((0, 0), (cols - HALF, 0), (0, 0)))
        o = o + jnp.pad(east[i].astype(f32), ((0, 0), (0, cols - HALF), (0, 0)))
        outs.append(o.astype(bf16))
    return outs


def window_start(first, row, total_rows):
    return jnp.minimum(jnp.maximum(first + row - HALF, 0), total_rows - WIN) - first + HALF


def attention_kernel(first_ref, q_ref, do_ref, kv_ref, dq_ref, dkv_ref, bias_ref, *, cols, ext_cols, total_rows, head_dim):
    nq = q_ref.shape[0]
    nk = kv_ref.shape[1]
    rows = nq // cols
    half = rows // 2
    bq = half * cols
    bk = (half + 2 * HALF) * ext_cols
    shift_k = half * ext_cols
    scale = 1.0 / math.sqrt(head_dim)
    f32 = jnp.float32
    nt = (((1,), (1,)), ((), ()))
    first = first_ref[0]

    @pl.when(pl.program_id(0) == 0)
    def _():
        qi = lax.broadcasted_iota(jnp.int32, (bq, bk), 0)
        ki = lax.broadcasted_iota(jnp.int32, (bq, bk), 1)
        rr = lax.shift_right_logical(qi, cols.bit_length() - 1)
        c = lax.bitwise_and(qi, cols - 1)
        i = lax.shift_right_logical(ki, ext_cols.bit_length() - 1)
        j = lax.bitwise_and(ki, ext_cols - 1)
        for blk in range(2):
            start = window_start(first, blk * half + rr, total_rows) - blk * half
            keep = (j >= c) & (j <= c + 2 * HALF) & (i >= start) & (i <= start + 2 * HALF)
            bias_ref[blk] = jnp.where(keep, 0.0, -1e30).astype(f32)

    pairs = q_ref.shape[1] // LANES
    lane = lax.broadcasted_iota(jnp.int32, (1, LANES), 1)
    lo = lane < head_dim
    sels = (lo, jnp.logical_not(lo))
    chains = [(blk, g, h) for blk in range(2) for g in range(pairs) for h in range(2)]
    qs = [slice(blk * bq, (blk + 1) * bq) for blk in range(2)]
    ks = [slice(blk * shift_k, blk * shift_k + bk) for blk in range(2)]
    gl = [slice(g * LANES, (g + 1) * LANES) for g in range(pairs)]
    q2 = [q_ref[:, gl[g]] for g in range(pairs)]
    do2 = [do_ref[:, gl[g]] for g in range(pairs)]
    qt = [q2[g].astype(f32).T.astype(jnp.bfloat16) for g in range(pairs)]
    dot_t = [do2[g].astype(f32).T.astype(jnp.bfloat16) for g in range(pairs)]
    k2 = {(blk, g): kv_ref[0, ks[blk], gl[g]] for blk in range(2) for g in range(pairs)}
    v2 = {(blk, g): kv_ref[1, ks[blk], gl[g]] for blk in range(2) for g in range(pairs)}
    qb = {(blk, g): q2[g][qs[blk]] for blk in range(2) for g in range(pairs)}
    dob = {(blk, g): do2[g][qs[blk]] for blk in range(2) for g in range(pairs)}
    sc = {}
    for blk, g, h in chains:
        qh = jnp.where(sels[h], qb[blk, g], jnp.zeros_like(qb[blk, g]))
        sc[blk, g, h] = lax.dot_general(qh, k2[blk, g], nt, preferred_element_type=f32)
    dps = {}
    for blk, g, h in chains:
        doh = jnp.where(sels[h], dob[blk, g], jnp.zeros_like(dob[blk, g]))
        dps[blk, g, h] = lax.dot_general(doh, v2[blk, g], nt, preferred_element_type=f32)
    probs, ws = {}, {}
    for c in chains:
        s = sc[c] * scale + bias_ref[c[0]]
        m = jnp.max(s, axis=1, keepdims=True)
        p = jnp.exp(s - m)
        l = jnp.sum(p, axis=1, keepdims=True)
        probs[c] = p * (1.0 / l)
        ws[c] = probs[c].astype(jnp.bfloat16)
    atts = {}
    for blk, g, h in chains:
        atts[blk, g, h] = jnp.dot(ws[blk, g, h], v2[blk, g], preferred_element_type=f32)
    dss = {}
    for blk, g, h in chains:
        c = (blk, g, h)
        delta = jnp.sum(jnp.where(sels[h], dob[blk, g].astype(f32) * atts[c], 0.0), axis=1, keepdims=True)
        dss[c] = (probs[c] * (dps[c] - delta) * scale).astype(jnp.bfloat16)
    dqs, dkt, dvt = {}, {}, {}
    for blk, g, h in chains:
        c = (blk, g, h)
        dims = slice(h * head_dim, (h + 1) * head_dim)
        dqs[c] = jnp.dot(dss[c], k2[blk, g], preferred_element_type=f32)
        dkt[c] = jnp.dot(qt[g][dims, qs[blk]], dss[c], preferred_element_type=f32)
        dvt[c] = jnp.dot(dot_t[g][dims, qs[blk]], ws[c], preferred_element_type=f32)
    for blk in range(2):
        for g in range(pairs):
            dq_ref[qs[blk], gl[g]] = jnp.where(lo, dqs[blk, g, 0], dqs[blk, g, 1]).astype(dq_ref.dtype)

    def joined(parts, g):
        heads = []
        for h in range(2):
            a, b = parts[0, g, h], parts[1, g, h]
            heads.append(
                jnp.concatenate(
                    [a[:, :shift_k], a[:, shift_k:] + b[:, : bk - shift_k], b[:, bk - shift_k :]], axis=1
                )
            )
        return jnp.concatenate(heads, axis=0).T

    for g in range(pairs):
        dkv_ref[0, :, gl[g]] = joined(dkt, g)
        dkv_ref[1, :, gl[g]] = joined(dvt, g)


def local_grads(first_row, q, do, kv, cols, ext_cols, total_rows):
    nq, width = q.shape
    nk = kv.shape[1]
    head_dim = width // HEADS
    step_lanes = LANES * STEP_PAIRS
    steps = width // step_lanes
    kern = functools.partial(
        attention_kernel, cols=cols, ext_cols=ext_cols, total_rows=total_rows, head_dim=head_dim
    )
    grid_spec = pltpu.PrefetchScalarGridSpec(
        num_scalar_prefetch=1,
        grid=(steps,),
        in_specs=[
            pl.BlockSpec((nq, step_lanes), lambda p, f: (0, p)),
            pl.BlockSpec((nq, step_lanes), lambda p, f: (0, p)),
            pl.BlockSpec((2, nk, step_lanes), lambda p, f: (0, 0, p)),
        ],
        out_specs=[
            pl.BlockSpec((nq, step_lanes), lambda p, f: (0, p)),
            pl.BlockSpec((2, nk, step_lanes), lambda p, f: (0, 0, p)),
        ],
        scratch_shapes=[pltpu.VMEM((2, nq // 2, nk - (nq // cols // 2) * ext_cols), jnp.float32)],
    )
    flops = 2 * nq * nk * LANES * 6 * HEADS
    cost = pl.CostEstimate(
        flops=flops,
        transcendentals=nq * nk * HEADS,
        bytes_accessed=2 * nq * width * 2 + 2 * nk * width * 2 + nq * width * 2 + 2 * nk * width * 4,
    )
    return pl.pallas_call(
        kern,
        grid_spec=grid_spec,
        out_shape=[
            jax.ShapeDtypeStruct((nq, width), jnp.bfloat16),
            jax.ShapeDtypeStruct((2, nk, width), jnp.float32),
        ],
        compiler_params=pltpu.CompilerParams(
            dimension_semantics=("arbitrary",), vmem_limit_bytes=48 * 1024 * 1024
        ),
        cost_estimate=cost,
    )(first_row, q, do, kv)


def per_device(queries, keys, values, d_out):
    rows, cols, width = queries.shape
    total_rows = rows * lax.axis_size("lat")
    first_row = (lax.axis_index("lat") * rows).astype(jnp.int32).reshape(1)
    pair = jnp.stack([keys, values])
    ext = gather_halo(pair)
    ext_rows, ext_cols = ext.shape[1], ext.shape[2]
    kv = ext.reshape(2, ext_rows * ext_cols, width)
    dq, dkv = local_grads(
        first_row,
        queries.reshape(rows * cols, width),
        d_out.reshape(rows * cols, width),
        kv,
        cols,
        ext_cols,
        total_rows,
    )
    d_keys, d_values = return_halo(dkv.reshape(2, ext_rows, ext_cols, width), rows, cols)
    return dq.reshape(rows, cols, width), d_keys, d_values


def solution(mesh):
    spec = P("lat", "lon", None)
    return jax.shard_map(
        per_device, mesh=mesh, in_specs=(spec,) * 4, out_specs=(spec,) * 3, check_vma=False
    )
```

```python
import functools
import math

import jax
import jax.numpy as jnp
from jax import lax
from jax.experimental import pallas as pl
from jax.experimental.pallas import tpu as pltpu
from jax.sharding import PartitionSpec as P

HEADS = 8
HALF = 6
WIN = 2 * HALF + 1
PAD_COLS = 4
LANES = 128
STEP_PAIRS = 2


def own_slice(d, n):
    return {-1: slice(n - HALF, n), 0: slice(0, n), 1: slice(0, HALF)}[d]


def halo_slice(d, n):
    return {-1: slice(0, HALF), 0: slice(HALF, HALF + n), 1: slice(HALF + n, 2 * HALF + n)}[d]


def shift(x, dr, dc):
    n_lat = lax.axis_size("lat")
    n_lon = lax.axis_size("lon")
    pairs = []
    for a in range(n_lat):
        if not 0 <= a + dr < n_lat:
            continue
        for b in range(n_lon):
            pairs.append((b * n_lat + a, ((b + dc) % n_lon) * n_lat + a + dr))
    flat = x.reshape(-1, x.shape[-1])
    return lax.ppermute(flat, ("lon", "lat"), pairs).reshape(x.shape)


def gather_halo(pair):
    _, rows, cols, _ = pair.shape
    left = shift(pair[:, :, own_slice(-1, cols)], 0, 1)
    right = shift(pair[:, :, own_slice(1, cols)], 0, -1)
    wide = jnp.concatenate([left, pair, right], axis=2)
    top = shift(wide[:, own_slice(-1, rows)], 1, 0)
    bottom = shift(wide[:, own_slice(1, rows)], -1, 0)
    ext = jnp.concatenate([top, wide, bottom], axis=1)
    return jnp.pad(ext, ((0, 0), (0, 0), (0, PAD_COLS), (0, 0)))


def return_halo(halo, band_rows, rows, cols):
    f32, bf16 = jnp.float32, jnp.bfloat16
    ec = slice(0, cols + 2 * HALF)
    up = shift(halo[:, 0, :, ec], -1, 0)
    down = shift(halo[:, 1, :, ec], 1, 0)

    def band(g, u, d, cs):
        b = g[:, :, cs]
        b = b + jnp.pad(u[:, :, cs].astype(f32), ((0, 0), (rows - HALF, 0), (0, 0), (0, 0)))
        return b + jnp.pad(d[:, :, cs].astype(f32), ((0, 0), (0, rows - HALF), (0, 0), (0, 0)))

    west_piece = band(band_rows, up, down, halo_slice(-1, cols)).astype(bf16)
    east_piece = band(band_rows, up, down, halo_slice(1, cols)).astype(bf16)
    west_piece, east_piece, band_rows, up, down = lax.optimization_barrier(
        (west_piece, east_piece, band_rows, up, down)
    )
    west = shift(west_piece, 0, -1)
    east = shift(east_piece, 0, 1)
    centre = band(band_rows, up, down, halo_slice(0, cols))
    outs = []
    for i in range(2):
        o = centre[i] + jnp.pad(west[i].astype(f32), ((0, 0), (cols - HALF, 0), (0, 0)))
        o = o + jnp.pad(east[i].astype(f32), ((0, 0), (0, cols - HALF), (0, 0)))
        outs.append(o.astype(bf16))
    return outs


def window_start(first, row, total_rows):
    return jnp.minimum(jnp.maximum(first + row - HALF, 0), total_rows - WIN) - first + HALF


def attention_kernel(
    first_ref, q_ref, do_ref, kv_ref, dq_ref, halo_ref, band_ref, bias_ref, *, cols, ext_cols, total_rows, head_dim
):
    nq = q_ref.shape[0]
    nk = kv_ref.shape[1]
    rows = nq // cols
    half = rows // 2
    bq = half * cols
    bk = (half + 2 * HALF) * ext_cols
    shift_k = half * ext_cols
    scale = 1.0 / math.sqrt(head_dim)
    f32 = jnp.float32
    nt = (((1,), (1,)), ((), ()))
    first = first_ref[0]

    @pl.when(pl.program_id(0) == 0)
    def _():
        qi = lax.broadcasted_iota(jnp.int32, (bq, bk), 0)
        ki = lax.broadcasted_iota(jnp.int32, (bq, bk), 1)
        rr = lax.shift_right_logical(qi, cols.bit_length() - 1)
        c = lax.bitwise_and(qi, cols - 1)
        i = lax.shift_right_logical(ki, ext_cols.bit_length() - 1)
        j = lax.bitwise_and(ki, ext_cols - 1)
        for blk in range(2):
            start = window_start(first, blk * half + rr, total_rows) - blk * half
            keep = (j >= c) & (j <= c + 2 * HALF) & (i >= start) & (i <= start + 2 * HALF)
            bias_ref[blk] = jnp.where(keep, 0.0, -1e30).astype(f32)

    pairs = q_ref.shape[1] // LANES
    lane = lax.broadcasted_iota(jnp.int32, (1, LANES), 1)
    lo = lane < head_dim
    sels = (lo, jnp.logical_not(lo))
    chains = [(blk, g, h) for blk in range(2) for g in range(pairs) for h in range(2)]
    qs = [slice(blk * bq, (blk + 1) * bq) for blk in range(2)]
    ks = [slice(blk * shift_k, blk * shift_k + bk) for blk in range(2)]
    gl = [slice(g * LANES, (g + 1) * LANES) for g in range(pairs)]
    q2 = [q_ref[:, gl[g]] for g in range(pairs)]
    do2 = [do_ref[:, gl[g]] for g in range(pairs)]
    qt = [q2[g].astype(f32).T.astype(jnp.bfloat16) for g in range(pairs)]
    dot_t = [do2[g].astype(f32).T.astype(jnp.bfloat16) for g in range(pairs)]
    k2 = {(blk, g): kv_ref[0, ks[blk], gl[g]] for blk in range(2) for g in range(pairs)}
    v2 = {(blk, g): kv_ref[1, ks[blk], gl[g]] for blk in range(2) for g in range(pairs)}
    qb = {(blk, g): q2[g][qs[blk]] for blk in range(2) for g in range(pairs)}
    dob = {(blk, g): do2[g][qs[blk]] for blk in range(2) for g in range(pairs)}
    sc = {}
    for blk, g, h in chains:
        qh = jnp.where(sels[h], qb[blk, g], jnp.zeros_like(qb[blk, g]))
        sc[blk, g, h] = lax.dot_general(qh, k2[blk, g], nt, preferred_element_type=f32)
    dps = {}
    for blk, g, h in chains:
        doh = jnp.where(sels[h], dob[blk, g], jnp.zeros_like(dob[blk, g]))
        dps[blk, g, h] = lax.dot_general(doh, v2[blk, g], nt, preferred_element_type=f32)
    probs, ws = {}, {}
    for c in chains:
        s = sc[c] * scale + bias_ref[c[0]]
        m = jnp.max(s, axis=1, keepdims=True)
        p = jnp.exp(s - m)
        l = jnp.sum(p, axis=1, keepdims=True)
        probs[c] = p * (1.0 / l)
        ws[c] = probs[c].astype(jnp.bfloat16)
    atts = {}
    for blk, g, h in chains:
        atts[blk, g, h] = jnp.dot(ws[blk, g, h], v2[blk, g], preferred_element_type=f32)
    dss = {}
    for blk, g, h in chains:
        c = (blk, g, h)
        delta = jnp.sum(jnp.where(sels[h], dob[blk, g].astype(f32) * atts[c], 0.0), axis=1, keepdims=True)
        dss[c] = (probs[c] * (dps[c] - delta) * scale).astype(jnp.bfloat16)
    dqs, dkt, dvt = {}, {}, {}
    for blk, g, h in chains:
        c = (blk, g, h)
        dims = slice(h * head_dim, (h + 1) * head_dim)
        dqs[c] = jnp.dot(dss[c], k2[blk, g], preferred_element_type=f32)
        dkt[c] = jnp.dot(qt[g][dims, qs[blk]], dss[c], preferred_element_type=f32)
        dvt[c] = jnp.dot(dot_t[g][dims, qs[blk]], ws[c], preferred_element_type=f32)
    for blk in range(2):
        for g in range(pairs):
            dq_ref[qs[blk], gl[g]] = jnp.where(lo, dqs[blk, g, 0], dqs[blk, g, 1]).astype(dq_ref.dtype)

    def joined(parts, g):
        heads = []
        for h in range(2):
            a, b = parts[0, g, h], parts[1, g, h]
            heads.append(
                jnp.concatenate(
                    [a[:, :shift_k], a[:, shift_k:] + b[:, : bk - shift_k], b[:, bk - shift_k :]], axis=1
                )
            )
        return jnp.concatenate(heads, axis=0).T

    edge = HALF * ext_cols
    for g in range(pairs):
        for i, parts in enumerate((dkt, dvt)):
            full = joined(parts, g)
            halo_ref[i, 0, :, gl[g]] = full[:edge].astype(halo_ref.dtype)
            halo_ref[i, 1, :, gl[g]] = full[nk - edge :].astype(halo_ref.dtype)
            band_ref[i, :, gl[g]] = full[edge : nk - edge]


def local_grads(first_row, q, do, kv, cols, ext_cols, total_rows):
    nq, width = q.shape
    nk = kv.shape[1]
    head_dim = width // HEADS
    step_lanes = LANES * STEP_PAIRS
    edge = HALF * ext_cols
    steps = width // step_lanes
    kern = functools.partial(
        attention_kernel, cols=cols, ext_cols=ext_cols, total_rows=total_rows, head_dim=head_dim
    )
    grid_spec = pltpu.PrefetchScalarGridSpec(
        num_scalar_prefetch=1,
        grid=(steps,),
        in_specs=[
            pl.BlockSpec((nq, step_lanes), lambda p, f: (0, p)),
            pl.BlockSpec((nq, step_lanes), lambda p, f: (0, p)),
            pl.BlockSpec((2, nk, step_lanes), lambda p, f: (0, 0, p)),
        ],
        out_specs=[
            pl.BlockSpec((nq, step_lanes), lambda p, f: (0, p)),
            pl.BlockSpec((2, 2, edge, step_lanes), lambda p, f: (0, 0, 0, p)),
            pl.BlockSpec((2, nk - 2 * edge, step_lanes), lambda p, f: (0, 0, p)),
        ],
        scratch_shapes=[pltpu.VMEM((2, nq // 2, nk - (nq // cols // 2) * ext_cols), jnp.float32)],
    )
    flops = 2 * nq * nk * LANES * 6 * HEADS
    cost = pl.CostEstimate(
        flops=flops,
        transcendentals=nq * nk * HEADS,
        bytes_accessed=2 * nq * width * 2 + 2 * nk * width * 2 + nq * width * 2 + 2 * nk * width * 4,
    )
    return pl.pallas_call(
        kern,
        grid_spec=grid_spec,
        out_shape=[
            jax.ShapeDtypeStruct((nq, width), jnp.bfloat16),
            jax.ShapeDtypeStruct((2, 2, edge, width), jnp.bfloat16),
            jax.ShapeDtypeStruct((2, nk - 2 * edge, width), jnp.float32),
        ],
        compiler_params=pltpu.CompilerParams(
            dimension_semantics=("arbitrary",), vmem_limit_bytes=48 * 1024 * 1024
        ),
        cost_estimate=cost,
    )(first_row, q, do, kv)


def per_device(queries, keys, values, d_out):
    rows, cols, width = queries.shape
    total_rows = rows * lax.axis_size("lat")
    first_row = (lax.axis_index("lat") * rows).astype(jnp.int32).reshape(1)
    pair = jnp.stack([keys, values])
    ext = gather_halo(pair)
    ext_rows, ext_cols = ext.shape[1], ext.shape[2]
    kv = ext.reshape(2, ext_rows * ext_cols, width)
    dq, halo, band_rows = local_grads(
        first_row,
        queries.reshape(rows * cols, width),
        d_out.reshape(rows * cols, width),
        kv,
        cols,
        ext_cols,
        total_rows,
    )
    d_keys, d_values = return_halo(
        halo.reshape(2, 2, HALF, ext_cols, width), band_rows.reshape(2, rows, ext_cols, width), rows, cols
    )
    return dq.reshape(rows, cols, width), d_keys, d_values


def solution(mesh):
    spec = P("lat", "lon", None)
    return jax.shard_map(
        per_device, mesh=mesh, in_specs=(spec,) * 4, out_specs=(spec,) * 3, check_vma=False
    )
```

```python
import functools
import math

import jax
import jax.numpy as jnp
from jax import lax
from jax.experimental import pallas as pl
from jax.experimental.pallas import tpu as pltpu
from jax.sharding import PartitionSpec as P

HEADS = 8
HALF = 6
WIN = 2 * HALF + 1
PAD_COLS = 4
LANES = 128
STEP_PAIRS = 4


def own_slice(d, n):
    return {-1: slice(n - HALF, n), 0: slice(0, n), 1: slice(0, HALF)}[d]


def halo_slice(d, n):
    return {-1: slice(0, HALF), 0: slice(HALF, HALF + n), 1: slice(HALF + n, 2 * HALF + n)}[d]


def shift(x, dr, dc):
    n_lat = lax.axis_size("lat")
    n_lon = lax.axis_size("lon")
    pairs = []
    for a in range(n_lat):
        if not 0 <= a + dr < n_lat:
            continue
        for b in range(n_lon):
            pairs.append((b * n_lat + a, ((b + dc) % n_lon) * n_lat + a + dr))
    flat = x.reshape(-1, x.shape[-1])
    return lax.ppermute(flat, ("lon", "lat"), pairs).reshape(x.shape)


def gather_halo(pair):
    _, rows, cols, _ = pair.shape
    left = shift(pair[:, :, own_slice(-1, cols)], 0, 1)
    right = shift(pair[:, :, own_slice(1, cols)], 0, -1)
    wide = jnp.concatenate([left, pair, right], axis=2)
    top = shift(wide[:, own_slice(-1, rows)], 1, 0)
    bottom = shift(wide[:, own_slice(1, rows)], -1, 0)
    ext = jnp.concatenate([top, wide, bottom], axis=1)
    return jnp.pad(ext, ((0, 0), (0, 0), (0, PAD_COLS), (0, 0)))


def return_halo(grads, rows, cols):
    f32, bf16 = jnp.float32, jnp.bfloat16
    ec = slice(0, cols + 2 * HALF)
    up = shift(grads[:, halo_slice(-1, rows), ec].astype(bf16), -1, 0)
    down = shift(grads[:, halo_slice(1, rows), ec].astype(bf16), 1, 0)

    def band(g, u, d, cs):
        b = g[:, HALF : HALF + rows, cs]
        b = b + jnp.pad(u[:, :, cs].astype(f32), ((0, 0), (rows - HALF, 0), (0, 0), (0, 0)))
        return b + jnp.pad(d[:, :, cs].astype(f32), ((0, 0), (0, rows - HALF), (0, 0), (0, 0)))

    west_piece = band(grads, up, down, halo_slice(-1, cols)).astype(bf16)
    east_piece = band(grads, up, down, halo_slice(1, cols)).astype(bf16)
    west_piece, east_piece, grads, up, down = lax.optimization_barrier((west_piece, east_piece, grads, up, down))
    west = shift(west_piece, 0, -1)
    east = shift(east_piece, 0, 1)
    centre = band(grads, up, down, halo_slice(0, cols))
    outs = []
    for i in range(2):
        o = centre[i] + jnp.pad(west[i].astype(f32), ((0, 0), (cols - HALF, 0), (0, 0)))
        o = o + jnp.pad(east[i].astype(f32), ((0, 0), (0, cols - HALF), (0, 0)))
        outs.append(o.astype(bf16))
    return outs


def window_start(first, row, total_rows):
    return jnp.minimum(jnp.maximum(first + row - HALF, 0), total_rows - WIN) - first + HALF


def attention_kernel(first_ref, q_ref, do_ref, kv_ref, dq_ref, dkv_ref, bias_ref, *, cols, ext_cols, total_rows, head_dim):
    nq = q_ref.shape[0]
    nk = kv_ref.shape[1]
    rows = nq // cols
    half = rows // 2
    bq = half * cols
    bk = (half + 2 * HALF) * ext_cols
    shift_k = half * ext_cols
    scale = 1.0 / math.sqrt(head_dim)
    f32 = jnp.float32
    nt = (((1,), (1,)), ((), ()))
    first = first_ref[0]

    @pl.when(pl.program_id(0) == 0)
    def _():
        qi = lax.broadcasted_iota(jnp.int32, (bq, bk), 0)
        ki = lax.broadcasted_iota(jnp.int32, (bq, bk), 1)
        rr = lax.shift_right_logical(qi, cols.bit_length() - 1)
        c = lax.bitwise_and(qi, cols - 1)
        i = lax.shift_right_logical(ki, ext_cols.bit_length() - 1)
        j = lax.bitwise_and(ki, ext_cols - 1)
        for blk in range(2):
            start = window_start(first, blk * half + rr, total_rows) - blk * half
            keep = (j >= c) & (j <= c + 2 * HALF) & (i >= start) & (i <= start + 2 * HALF)
            bias_ref[blk] = jnp.where(keep, 0.0, -1e30).astype(f32)

    pairs = q_ref.shape[1] // LANES
    lane = lax.broadcasted_iota(jnp.int32, (1, LANES), 1)
    lo = lane < head_dim
    sels = (lo, jnp.logical_not(lo))
    chains = [(blk, g, h) for blk in range(2) for g in range(pairs) for h in range(2)]
    qs = [slice(blk * bq, (blk + 1) * bq) for blk in range(2)]
    ks = [slice(blk * shift_k, blk * shift_k + bk) for blk in range(2)]
    gl = [slice(g * LANES, (g + 1) * LANES) for g in range(pairs)]
    q2 = [q_ref[:, gl[g]] for g in range(pairs)]
    do2 = [do_ref[:, gl[g]] for g in range(pairs)]
    qt = [q2[g].astype(f32).T.astype(jnp.bfloat16) for g in range(pairs)]
    dot_t = [do2[g].astype(f32).T.astype(jnp.bfloat16) for g in range(pairs)]
    k2 = {(blk, g): kv_ref[0, ks[blk], gl[g]] for blk in range(2) for g in range(pairs)}
    v2 = {(blk, g): kv_ref[1, ks[blk], gl[g]] for blk in range(2) for g in range(pairs)}
    qb = {(blk, g): q2[g][qs[blk]] for blk in range(2) for g in range(pairs)}
    dob = {(blk, g): do2[g][qs[blk]] for blk in range(2) for g in range(pairs)}
    sc = {}
    for blk, g, h in chains:
        qh = jnp.where(sels[h], qb[blk, g], jnp.zeros_like(qb[blk, g]))
        sc[blk, g, h] = lax.dot_general(qh, k2[blk, g], nt, preferred_element_type=f32)
    dps = {}
    for blk, g, h in chains:
        doh = jnp.where(sels[h], dob[blk, g], jnp.zeros_like(dob[blk, g]))
        dps[blk, g, h] = lax.dot_general(doh, v2[blk, g], nt, preferred_element_type=f32)
    probs, ws = {}, {}
    for c in chains:
        s = sc[c] * scale + bias_ref[c[0]]
        m = jnp.max(s, axis=1, keepdims=True)
        p = jnp.exp(s - m)
        l = jnp.sum(p, axis=1, keepdims=True)
        probs[c] = p * (1.0 / l)
        ws[c] = probs[c].astype(jnp.bfloat16)
    atts = {}
    for blk, g, h in chains:
        atts[blk, g, h] = jnp.dot(ws[blk, g, h], v2[blk, g], preferred_element_type=f32)
    dss = {}
    for blk, g, h in chains:
        c = (blk, g, h)
        delta = jnp.sum(jnp.where(sels[h], dob[blk, g].astype(f32) * atts[c], 0.0), axis=1, keepdims=True)
        dss[c] = (probs[c] * (dps[c] - delta) * scale).astype(jnp.bfloat16)
    dqs, dkt, dvt = {}, {}, {}
    for blk, g, h in chains:
        c = (blk, g, h)
        dims = slice(h * head_dim, (h + 1) * head_dim)
        dqs[c] = jnp.dot(dss[c], k2[blk, g], preferred_element_type=f32)
        dkt[c] = jnp.dot(qt[g][dims, qs[blk]], dss[c], preferred_element_type=f32)
        dvt[c] = jnp.dot(dot_t[g][dims, qs[blk]], ws[c], preferred_element_type=f32)
    for blk in range(2):
        for g in range(pairs):
            dq_ref[qs[blk], gl[g]] = jnp.where(lo, dqs[blk, g, 0], dqs[blk, g, 1]).astype(dq_ref.dtype)

    def joined(parts, g):
        heads = []
        for h in range(2):
            a, b = parts[0, g, h], parts[1, g, h]
            heads.append(
                jnp.concatenate(
                    [a[:, :shift_k], a[:, shift_k:] + b[:, : bk - shift_k], b[:, bk - shift_k :]], axis=1
                )
            )
        return jnp.concatenate(heads, axis=0).T

    for g in range(pairs):
        dkv_ref[0, :, gl[g]] = joined(dkt, g)
        dkv_ref[1, :, gl[g]] = joined(dvt, g)


def local_grads(first_row, q, do, kv, cols, ext_cols, total_rows):
    nq, width = q.shape
    nk = kv.shape[1]
    head_dim = width // HEADS
    step_lanes = LANES * STEP_PAIRS
    steps = width // step_lanes
    kern = functools.partial(
        attention_kernel, cols=cols, ext_cols=ext_cols, total_rows=total_rows, head_dim=head_dim
    )
    grid_spec = pltpu.PrefetchScalarGridSpec(
        num_scalar_prefetch=1,
        grid=(steps,),
        in_specs=[
            pl.BlockSpec((nq, step_lanes), lambda p, f: (0, p)),
            pl.BlockSpec((nq, step_lanes), lambda p, f: (0, p)),
            pl.BlockSpec((2, nk, step_lanes), lambda p, f: (0, 0, p)),
        ],
        out_specs=[
            pl.BlockSpec((nq, step_lanes), lambda p, f: (0, p)),
            pl.BlockSpec((2, nk, step_lanes), lambda p, f: (0, 0, p)),
        ],
        scratch_shapes=[pltpu.VMEM((2, nq // 2, nk - (nq // cols // 2) * ext_cols), jnp.float32)],
    )
    flops = 2 * nq * nk * LANES * 6 * HEADS
    cost = pl.CostEstimate(
        flops=flops,
        transcendentals=nq * nk * HEADS,
        bytes_accessed=2 * nq * width * 2 + 2 * nk * width * 2 + nq * width * 2 + 2 * nk * width * 4,
    )
    return pl.pallas_call(
        kern,
        grid_spec=grid_spec,
        out_shape=[
            jax.ShapeDtypeStruct((nq, width), jnp.bfloat16),
            jax.ShapeDtypeStruct((2, nk, width), jnp.float32),
        ],
        compiler_params=pltpu.CompilerParams(
            dimension_semantics=("arbitrary",), vmem_limit_bytes=48 * 1024 * 1024
        ),
        cost_estimate=cost,
    )(first_row, q, do, kv)


def per_device(queries, keys, values, d_out):
    rows, cols, width = queries.shape
    total_rows = rows * lax.axis_size("lat")
    first_row = (lax.axis_index("lat") * rows).astype(jnp.int32).reshape(1)
    pair = jnp.stack([keys, values])
    ext = gather_halo(pair)
    ext_rows, ext_cols = ext.shape[1], ext.shape[2]
    kv = ext.reshape(2, ext_rows * ext_cols, width)
    dq, dkv = local_grads(
        first_row,
        queries.reshape(rows * cols, width),
        d_out.reshape(rows * cols, width),
        kv,
        cols,
        ext_cols,
        total_rows,
    )
    d_keys, d_values = return_halo(dkv.reshape(2, ext_rows, ext_cols, width), rows, cols)
    return dq.reshape(rows, cols, width), d_keys, d_values


def solution(mesh):
    spec = P("lat", "lon", None)
    return jax.shard_map(
        per_device, mesh=mesh, in_specs=(spec,) * 4, out_specs=(spec,) * 3, check_vma=False
    )
```

```python
import functools
import math

import jax
import jax.numpy as jnp
from jax import lax
from jax.experimental import pallas as pl
from jax.experimental.pallas import tpu as pltpu
from jax.sharding import PartitionSpec as P

HEADS = 8
HALF = 6
WIN = 2 * HALF + 1
PAD_COLS = 4
LANES = 128
STEP_PAIRS = 4


def own_slice(d, n):
    return {-1: slice(n - HALF, n), 0: slice(0, n), 1: slice(0, HALF)}[d]


def halo_slice(d, n):
    return {-1: slice(0, HALF), 0: slice(HALF, HALF + n), 1: slice(HALF + n, 2 * HALF + n)}[d]


def shift(x, dr, dc):
    n_lat = lax.axis_size("lat")
    n_lon = lax.axis_size("lon")
    pairs = []
    for a in range(n_lat):
        if not 0 <= a + dr < n_lat:
            continue
        for b in range(n_lon):
            pairs.append((b * n_lat + a, ((b + dc) % n_lon) * n_lat + a + dr))
    flat = x.reshape(-1, x.shape[-1])
    return lax.ppermute(flat, ("lon", "lat"), pairs).reshape(x.shape)


def gather_halo(pair):
    _, rows, cols, _ = pair.shape
    left = shift(pair[:, :, own_slice(-1, cols)], 0, 1)
    right = shift(pair[:, :, own_slice(1, cols)], 0, -1)
    wide = jnp.concatenate([left, pair, right], axis=2)
    top = shift(wide[:, own_slice(-1, rows)], 1, 0)
    bottom = shift(wide[:, own_slice(1, rows)], -1, 0)
    ext = jnp.concatenate([top, wide, bottom], axis=1)
    return jnp.pad(ext, ((0, 0), (0, 0), (0, PAD_COLS), (0, 0)))


def return_halo(grads, rows, cols):
    f32, bf16 = jnp.float32, jnp.bfloat16
    ec = slice(0, cols + 2 * HALF)
    up = shift(grads[:, halo_slice(-1, rows), ec].astype(bf16), -1, 0)
    down = shift(grads[:, halo_slice(1, rows), ec].astype(bf16), 1, 0)

    def band(g, u, d, cs):
        b = g[:, HALF : HALF + rows, cs].astype(f32)
        b = b + jnp.pad(u[:, :, cs].astype(f32), ((0, 0), (rows - HALF, 0), (0, 0), (0, 0)))
        return b + jnp.pad(d[:, :, cs].astype(f32), ((0, 0), (0, rows - HALF), (0, 0), (0, 0)))

    west_piece = band(grads, up, down, halo_slice(-1, cols)).astype(bf16)
    east_piece = band(grads, up, down, halo_slice(1, cols)).astype(bf16)
    west_piece, east_piece, grads, up, down = lax.optimization_barrier((west_piece, east_piece, grads, up, down))
    west = shift(west_piece, 0, -1)
    east = shift(east_piece, 0, 1)
    centre = band(grads, up, down, halo_slice(0, cols))
    outs = []
    for i in range(2):
        o = centre[i] + jnp.pad(west[i].astype(f32), ((0, 0), (cols - HALF, 0), (0, 0)))
        o = o + jnp.pad(east[i].astype(f32), ((0, 0), (0, cols - HALF), (0, 0)))
        outs.append(o.astype(bf16))
    return outs


def window_start(first, row, total_rows):
    return jnp.minimum(jnp.maximum(first + row - HALF, 0), total_rows - WIN) - first + HALF


def attention_kernel(first_ref, q_ref, do_ref, kv_ref, dq_ref, dkv_ref, bias_ref, *, cols, ext_cols, total_rows, head_dim):
    nq = q_ref.shape[0]
    nk = kv_ref.shape[1]
    rows = nq // cols
    half = rows // 2
    bq = half * cols
    bk = (half + 2 * HALF) * ext_cols
    shift_k = half * ext_cols
    scale = 1.0 / math.sqrt(head_dim)
    f32 = jnp.float32
    nt = (((1,), (1,)), ((), ()))
    first = first_ref[0]

    @pl.when(pl.program_id(0) == 0)
    def _():
        qi = lax.broadcasted_iota(jnp.int32, (bq, bk), 0)
        ki = lax.broadcasted_iota(jnp.int32, (bq, bk), 1)
        rr = lax.shift_right_logical(qi, cols.bit_length() - 1)
        c = lax.bitwise_and(qi, cols - 1)
        i = lax.shift_right_logical(ki, ext_cols.bit_length() - 1)
        j = lax.bitwise_and(ki, ext_cols - 1)
        for blk in range(2):
            start = window_start(first, blk * half + rr, total_rows) - blk * half
            keep = (j >= c) & (j <= c + 2 * HALF) & (i >= start) & (i <= start + 2 * HALF)
            bias_ref[blk] = jnp.where(keep, 0.0, -1e30).astype(f32)

    pairs = q_ref.shape[1] // LANES
    lane = lax.broadcasted_iota(jnp.int32, (1, LANES), 1)
    lo = lane < head_dim
    sels = (lo, jnp.logical_not(lo))
    chains = [(blk, g, h) for blk in range(2) for g in range(pairs) for h in range(2)]
    qs = [slice(blk * bq, (blk + 1) * bq) for blk in range(2)]
    ks = [slice(blk * shift_k, blk * shift_k + bk) for blk in range(2)]
    gl = [slice(g * LANES, (g + 1) * LANES) for g in range(pairs)]
    q2 = [q_ref[:, gl[g]] for g in range(pairs)]
    do2 = [do_ref[:, gl[g]] for g in range(pairs)]
    qt = [q2[g].astype(f32).T.astype(jnp.bfloat16) for g in range(pairs)]
    dot_t = [do2[g].astype(f32).T.astype(jnp.bfloat16) for g in range(pairs)]
    k2 = {(blk, g): kv_ref[0, ks[blk], gl[g]] for blk in range(2) for g in range(pairs)}
    v2 = {(blk, g): kv_ref[1, ks[blk], gl[g]] for blk in range(2) for g in range(pairs)}
    qb = {(blk, g): q2[g][qs[blk]] for blk in range(2) for g in range(pairs)}
    dob = {(blk, g): do2[g][qs[blk]] for blk in range(2) for g in range(pairs)}
    sc = {}
    for blk, g, h in chains:
        qh = jnp.where(sels[h], qb[blk, g], jnp.zeros_like(qb[blk, g]))
        sc[blk, g, h] = lax.dot_general(qh, k2[blk, g], nt, preferred_element_type=f32)
    dps = {}
    for blk, g, h in chains:
        doh = jnp.where(sels[h], dob[blk, g], jnp.zeros_like(dob[blk, g]))
        dps[blk, g, h] = lax.dot_general(doh, v2[blk, g], nt, preferred_element_type=f32)
    probs, ws = {}, {}
    for c in chains:
        s = sc[c] * scale + bias_ref[c[0]]
        m = jnp.max(s, axis=1, keepdims=True)
        p = jnp.exp(s - m)
        l = jnp.sum(p, axis=1, keepdims=True)
        probs[c] = p * (1.0 / l)
        ws[c] = probs[c].astype(jnp.bfloat16)
    atts = {}
    for blk, g, h in chains:
        atts[blk, g, h] = jnp.dot(ws[blk, g, h], v2[blk, g], preferred_element_type=f32)
    dss = {}
    for blk, g, h in chains:
        c = (blk, g, h)
        delta = jnp.sum(jnp.where(sels[h], dob[blk, g].astype(f32) * atts[c], 0.0), axis=1, keepdims=True)
        dss[c] = (probs[c] * (dps[c] - delta) * scale).astype(jnp.bfloat16)
    dqs, dkt, dvt = {}, {}, {}
    for blk, g, h in chains:
        c = (blk, g, h)
        dims = slice(h * head_dim, (h + 1) * head_dim)
        dqs[c] = jnp.dot(dss[c], k2[blk, g], preferred_element_type=f32)
        dkt[c] = jnp.dot(qt[g][dims, qs[blk]], dss[c], preferred_element_type=f32)
        dvt[c] = jnp.dot(dot_t[g][dims, qs[blk]], ws[c], preferred_element_type=f32)
    for blk in range(2):
        for g in range(pairs):
            dq_ref[qs[blk], gl[g]] = jnp.where(lo, dqs[blk, g, 0], dqs[blk, g, 1]).astype(dq_ref.dtype)

    def joined(parts, g):
        heads = []
        for h in range(2):
            a, b = parts[0, g, h], parts[1, g, h]
            heads.append(
                jnp.concatenate(
                    [a[:, :shift_k], a[:, shift_k:] + b[:, : bk - shift_k], b[:, bk - shift_k :]], axis=1
                )
            )
        return jnp.concatenate(heads, axis=0).T

    for g in range(pairs):
        dkv_ref[0, :, gl[g]] = joined(dkt, g).astype(dkv_ref.dtype)
        dkv_ref[1, :, gl[g]] = joined(dvt, g).astype(dkv_ref.dtype)


def local_grads(first_row, q, do, kv, cols, ext_cols, total_rows):
    nq, width = q.shape
    nk = kv.shape[1]
    head_dim = width // HEADS
    step_lanes = LANES * STEP_PAIRS
    steps = width // step_lanes
    kern = functools.partial(
        attention_kernel, cols=cols, ext_cols=ext_cols, total_rows=total_rows, head_dim=head_dim
    )
    grid_spec = pltpu.PrefetchScalarGridSpec(
        num_scalar_prefetch=1,
        grid=(steps,),
        in_specs=[
            pl.BlockSpec((nq, step_lanes), lambda p, f: (0, p)),
            pl.BlockSpec((nq, step_lanes), lambda p, f: (0, p)),
            pl.BlockSpec((2, nk, step_lanes), lambda p, f: (0, 0, p)),
        ],
        out_specs=[
            pl.BlockSpec((nq, step_lanes), lambda p, f: (0, p)),
            pl.BlockSpec((2, nk, step_lanes), lambda p, f: (0, 0, p)),
        ],
        scratch_shapes=[pltpu.VMEM((2, nq // 2, nk - (nq // cols // 2) * ext_cols), jnp.float32)],
    )
    flops = 2 * nq * nk * LANES * 6 * HEADS
    cost = pl.CostEstimate(
        flops=flops,
        transcendentals=nq * nk * HEADS,
        bytes_accessed=2 * nq * width * 2 + 2 * nk * width * 2 + nq * width * 2 + 2 * nk * width * 4,
    )
    return pl.pallas_call(
        kern,
        grid_spec=grid_spec,
        out_shape=[
            jax.ShapeDtypeStruct((nq, width), jnp.bfloat16),
            jax.ShapeDtypeStruct((2, nk, width), jnp.bfloat16),
        ],
        compiler_params=pltpu.CompilerParams(
            dimension_semantics=("arbitrary",), vmem_limit_bytes=48 * 1024 * 1024
        ),
        cost_estimate=cost,
    )(first_row, q, do, kv)


def per_device(queries, keys, values, d_out):
    rows, cols, width = queries.shape
    total_rows = rows * lax.axis_size("lat")
    first_row = (lax.axis_index("lat") * rows).astype(jnp.int32).reshape(1)
    pair = jnp.stack([keys, values])
    ext = gather_halo(pair)
    ext_rows, ext_cols = ext.shape[1], ext.shape[2]
    kv = ext.reshape(2, ext_rows * ext_cols, width)
    dq, dkv = local_grads(
        first_row,
        queries.reshape(rows * cols, width),
        d_out.reshape(rows * cols, width),
        kv,
        cols,
        ext_cols,
        total_rows,
    )
    d_keys, d_values = return_halo(dkv.reshape(2, ext_rows, ext_cols, width), rows, cols)
    return dq.reshape(rows, cols, width), d_keys, d_values


def solution(mesh):
    spec = P("lat", "lon", None)
    return jax.shard_map(
        per_device, mesh=mesh, in_specs=(spec,) * 4, out_specs=(spec,) * 3, check_vma=False
    )
```

```python
import functools
import math

import jax
import jax.numpy as jnp
from jax import lax
from jax.experimental import pallas as pl
from jax.experimental.pallas import tpu as pltpu
from jax.sharding import PartitionSpec as P

HEADS = 8
HALF = 6
WIN = 2 * HALF + 1
PAD_COLS = 4
LANES = 128
STEP_PAIRS = 4


def own_slice(d, n):
    return {-1: slice(n - HALF, n), 0: slice(0, n), 1: slice(0, HALF)}[d]


def halo_slice(d, n):
    return {-1: slice(0, HALF), 0: slice(HALF, HALF + n), 1: slice(HALF + n, 2 * HALF + n)}[d]


def shift(x, dr, dc):
    n_lat = lax.axis_size("lat")
    n_lon = lax.axis_size("lon")
    pairs = []
    for a in range(n_lat):
        if not 0 <= a + dr < n_lat:
            continue
        for b in range(n_lon):
            pairs.append((b * n_lat + a, ((b + dc) % n_lon) * n_lat + a + dr))
    flat = x.reshape(-1, x.shape[-1])
    return lax.ppermute(flat, ("lon", "lat"), pairs).reshape(x.shape)


def gather_halo(pair):
    _, rows, cols, _ = pair.shape
    left = shift(pair[:, :, own_slice(-1, cols)], 0, 1)
    right = shift(pair[:, :, own_slice(1, cols)], 0, -1)
    wide = jnp.concatenate([left, pair, right], axis=2)
    top = shift(wide[:, own_slice(-1, rows)], 1, 0)
    bottom = shift(wide[:, own_slice(1, rows)], -1, 0)
    ext = jnp.concatenate([top, wide, bottom], axis=1)
    return jnp.pad(ext, ((0, 0), (0, 0), (0, PAD_COLS), (0, 0)))


def return_halo(grads, rows, cols):
    f32, bf16 = jnp.float32, jnp.bfloat16
    ec = slice(0, cols + 2 * HALF)
    up = shift(grads[:, halo_slice(-1, rows), ec].astype(bf16), -1, 0)
    down = shift(grads[:, halo_slice(1, rows), ec].astype(bf16), 1, 0)

    def band(g, u, d, cs):
        b = g[:, HALF : HALF + rows, cs].astype(f32)
        b = b + jnp.pad(u[:, :, cs].astype(f32), ((0, 0), (rows - HALF, 0), (0, 0), (0, 0)))
        return b + jnp.pad(d[:, :, cs].astype(f32), ((0, 0), (0, rows - HALF), (0, 0), (0, 0)))

    west_piece = band(grads, up, down, halo_slice(-1, cols)).astype(bf16)
    east_piece = band(grads, up, down, halo_slice(1, cols)).astype(bf16)
    west_piece, east_piece, grads, up, down = lax.optimization_barrier((west_piece, east_piece, grads, up, down))
    west = shift(west_piece, 0, -1)
    east = shift(east_piece, 0, 1)
    centre = band(grads, up, down, halo_slice(0, cols))
    outs = []
    for i in range(2):
        o = centre[i] + jnp.pad(west[i].astype(f32), ((0, 0), (cols - HALF, 0), (0, 0)))
        o = o + jnp.pad(east[i].astype(f32), ((0, 0), (0, cols - HALF), (0, 0)))
        outs.append(o.astype(bf16))
    return outs


def window_start(first, row, total_rows):
    return jnp.minimum(jnp.maximum(first + row - HALF, 0), total_rows - WIN) - first + HALF


def window_bias(first, rows, cols, ext_cols, total_rows):
    half = rows // 2
    bq = half * cols
    bk = (half + 2 * HALF) * ext_cols
    qi = lax.broadcasted_iota(jnp.int32, (bq, bk), 0)
    ki = lax.broadcasted_iota(jnp.int32, (bq, bk), 1)
    rr, c = qi // cols, qi % cols
    i, j = ki // ext_cols, ki % ext_cols
    out = []
    for blk in range(2):
        start = window_start(first, blk * half + rr, total_rows) - blk * half
        keep = (j >= c) & (j <= c + 2 * HALF) & (i >= start) & (i <= start + 2 * HALF)
        out.append(jnp.where(keep, 0.0, -1e30).astype(jnp.float32))
    return jnp.stack(out)


def attention_kernel(first_ref, q_ref, do_ref, kv_ref, bias_ref, dq_ref, dkv_ref, *, cols, ext_cols, total_rows, head_dim):
    nq = q_ref.shape[0]
    nk = kv_ref.shape[1]
    rows = nq // cols
    half = rows // 2
    bq = half * cols
    bk = (half + 2 * HALF) * ext_cols
    shift_k = half * ext_cols
    scale = 1.0 / math.sqrt(head_dim)
    f32 = jnp.float32
    nt = (((1,), (1,)), ((), ()))
    first = first_ref[0]

    pairs = q_ref.shape[1] // LANES
    lane = lax.broadcasted_iota(jnp.int32, (1, LANES), 1)
    lo = lane < head_dim
    sels = (lo, jnp.logical_not(lo))
    chains = [(blk, g, h) for blk in range(2) for g in range(pairs) for h in range(2)]
    qs = [slice(blk * bq, (blk + 1) * bq) for blk in range(2)]
    ks = [slice(blk * shift_k, blk * shift_k + bk) for blk in range(2)]
    gl = [slice(g * LANES, (g + 1) * LANES) for g in range(pairs)]
    q2 = [q_ref[:, gl[g]] for g in range(pairs)]
    do2 = [do_ref[:, gl[g]] for g in range(pairs)]
    qt = [q2[g].astype(f32).T.astype(jnp.bfloat16) for g in range(pairs)]
    dot_t = [do2[g].astype(f32).T.astype(jnp.bfloat16) for g in range(pairs)]
    k2 = {(blk, g): kv_ref[0, ks[blk], gl[g]] for blk in range(2) for g in range(pairs)}
    v2 = {(blk, g): kv_ref[1, ks[blk], gl[g]] for blk in range(2) for g in range(pairs)}
    qb = {(blk, g): q2[g][qs[blk]] for blk in range(2) for g in range(pairs)}
    dob = {(blk, g): do2[g][qs[blk]] for blk in range(2) for g in range(pairs)}
    sc = {}
    for blk, g, h in chains:
        qh = jnp.where(sels[h], qb[blk, g], jnp.zeros_like(qb[blk, g]))
        sc[blk, g, h] = lax.dot_general(qh, k2[blk, g], nt, preferred_element_type=f32)
    dps = {}
    for blk, g, h in chains:
        doh = jnp.where(sels[h], dob[blk, g], jnp.zeros_like(dob[blk, g]))
        dps[blk, g, h] = lax.dot_general(doh, v2[blk, g], nt, preferred_element_type=f32)
    probs, ws = {}, {}
    for c in chains:
        s = sc[c] * scale + bias_ref[c[0]]
        m = jnp.max(s, axis=1, keepdims=True)
        p = jnp.exp(s - m)
        l = jnp.sum(p, axis=1, keepdims=True)
        probs[c] = p * (1.0 / l)
        ws[c] = probs[c].astype(jnp.bfloat16)
    atts = {}
    for blk, g, h in chains:
        atts[blk, g, h] = jnp.dot(ws[blk, g, h], v2[blk, g], preferred_element_type=f32)
    dss = {}
    for blk, g, h in chains:
        c = (blk, g, h)
        delta = jnp.sum(jnp.where(sels[h], dob[blk, g].astype(f32) * atts[c], 0.0), axis=1, keepdims=True)
        dss[c] = (probs[c] * (dps[c] - delta) * scale).astype(jnp.bfloat16)
    dqs, dkt, dvt = {}, {}, {}
    for blk, g, h in chains:
        c = (blk, g, h)
        dims = slice(h * head_dim, (h + 1) * head_dim)
        dqs[c] = jnp.dot(dss[c], k2[blk, g], preferred_element_type=f32)
        dkt[c] = jnp.dot(qt[g][dims, qs[blk]], dss[c], preferred_element_type=f32)
        dvt[c] = jnp.dot(dot_t[g][dims, qs[blk]], ws[c], preferred_element_type=f32)
    for blk in range(2):
        for g in range(pairs):
            dq_ref[qs[blk], gl[g]] = jnp.where(lo, dqs[blk, g, 0], dqs[blk, g, 1]).astype(dq_ref.dtype)

    def joined(parts, g):
        heads = []
        for h in range(2):
            a, b = parts[0, g, h], parts[1, g, h]
            heads.append(
                jnp.concatenate(
                    [a[:, :shift_k], a[:, shift_k:] + b[:, : bk - shift_k], b[:, bk - shift_k :]], axis=1
                )
            )
        return jnp.concatenate(heads, axis=0).T

    for g in range(pairs):
        dkv_ref[0, :, gl[g]] = joined(dkt, g).astype(dkv_ref.dtype)
        dkv_ref[1, :, gl[g]] = joined(dvt, g).astype(dkv_ref.dtype)


def local_grads(first_row, q, do, kv, cols, ext_cols, total_rows):
    nq, width = q.shape
    nk = kv.shape[1]
    head_dim = width // HEADS
    step_lanes = LANES * STEP_PAIRS
    steps = width // step_lanes
    bias = window_bias(first_row[0], nq // cols, cols, ext_cols, total_rows)
    kern = functools.partial(
        attention_kernel, cols=cols, ext_cols=ext_cols, total_rows=total_rows, head_dim=head_dim
    )
    grid_spec = pltpu.PrefetchScalarGridSpec(
        num_scalar_prefetch=1,
        grid=(steps,),
        in_specs=[
            pl.BlockSpec((nq, step_lanes), lambda p, f: (0, p)),
            pl.BlockSpec((nq, step_lanes), lambda p, f: (0, p)),
            pl.BlockSpec((2, nk, step_lanes), lambda p, f: (0, 0, p)),
            pl.BlockSpec(bias.shape, lambda p, f: (0, 0, 0)),
        ],
        out_specs=[
            pl.BlockSpec((nq, step_lanes), lambda p, f: (0, p)),
            pl.BlockSpec((2, nk, step_lanes), lambda p, f: (0, 0, p)),
        ],
    )
    flops = 2 * nq * nk * LANES * 6 * HEADS
    cost = pl.CostEstimate(
        flops=flops,
        transcendentals=nq * nk * HEADS,
        bytes_accessed=2 * nq * width * 2 + 2 * nk * width * 2 + nq * width * 2 + 2 * nk * width * 4,
    )
    return pl.pallas_call(
        kern,
        grid_spec=grid_spec,
        out_shape=[
            jax.ShapeDtypeStruct((nq, width), jnp.bfloat16),
            jax.ShapeDtypeStruct((2, nk, width), jnp.bfloat16),
        ],
        compiler_params=pltpu.CompilerParams(
            dimension_semantics=("arbitrary",), vmem_limit_bytes=48 * 1024 * 1024
        ),
        cost_estimate=cost,
    )(first_row, q, do, kv, bias)


def per_device(queries, keys, values, d_out):
    rows, cols, width = queries.shape
    total_rows = rows * lax.axis_size("lat")
    first_row = (lax.axis_index("lat") * rows).astype(jnp.int32).reshape(1)
    pair = jnp.stack([keys, values])
    ext = gather_halo(pair)
    ext_rows, ext_cols = ext.shape[1], ext.shape[2]
    kv = ext.reshape(2, ext_rows * ext_cols, width)
    dq, dkv = local_grads(
        first_row,
        queries.reshape(rows * cols, width),
        d_out.reshape(rows * cols, width),
        kv,
        cols,
        ext_cols,
        total_rows,
    )
    d_keys, d_values = return_halo(dkv.reshape(2, ext_rows, ext_cols, width), rows, cols)
    return dq.reshape(rows, cols, width), d_keys, d_values


def solution(mesh):
    spec = P("lat", "lon", None)
    return jax.shard_map(
        per_device, mesh=mesh, in_specs=(spec,) * 4, out_specs=(spec,) * 3, check_vma=False
    )
```
